256 devices in a mesh: seq: 64 (over y, z, core), tr: 2 (over x_lo), tc: 2 (over x_hi).
Axes of the slice: x: 4 (x_hi: 2, x_lo: 2; x = x_hi * 2 + x_lo), y: 4, z: 8, core: 2. Of those that a mesh axis runs over, the one named last changes fastest.
Arguments:
- activations: bfloat16 [65536, 1024], P('seq', ('tr', 'tc')), may hold values from -6 to 6
- seg_len: int32 [64], P('seq'), may hold values from 1 to 1024, as said below
- seg_start: int32 [64], P('seq'), may hold values from 0 to 1, as said below
- memory_rates: float32 [3, 64, 8], P(None, 'seq'), may hold values from 0 to 1, as said below
- w_qkv: bfloat16 [1024, 3, 1024], P(None, None, ('tr', 'tc')), may hold values from -0.1875 to 0.1875
- conv_w: float32 [4, 3, 1024], P(None, None, ('tr', 'tc')), may hold values from -3 to 3
- persistent: bfloat16 [2, 16, 1024], P(None, None, ('tr', 'tc')), may hold values from -6 to 6
- w_out: bfloat16 [1024, 1024], P(('tr', 'tc')), may hold values from -0.1875 to 0.1875
- w_gate: bfloat16 [1024, 2816], P(None, ('tr', 'tc')), may hold values from -0.1875 to 0.1875
- w_up: bfloat16 [1024, 2816], P(None, ('tr', 'tc')), may hold values from -0.1875 to 0.1875
- w_down: bfloat16 [2816, 1024], P(('tr', 'tc')), may hold values from -0.109375 to 0.109375
Outputs:
- layer_out: bfloat16 [65536, 1024], P('seq', ('tr', 'tc'))
The draws below stay inside these ranges and needn't reach their ends.
Inputs may be any that keep to these rules, and one draw needn't show every extreme that they name: `seg_start`: 1 where a segment begins a prompt, 0 where it continues the prompt of the segment before; segment 0 begins a prompt; a prompt spans at most 32 segments, and in every draw one prompt spans exactly that many. `seg_len`: live tokens at the head of each segment; every segment of a prompt but its last is full. `memory_rates`: all three tables lie strictly between 0 and 1.
All inputs are finite; a program needn't handle non-finite values.
Results may differ from the reference program's by a relative error of at most 0.015.
Values may be sent and summed in bfloat16 or wider, within the bound.
No kernel may reach another device: no remote copies, remote signals or barrier semaphores. Data moves between devices by JAX's collectives and lax.ppermute only.
A program may use at most 192 MiB of HBM per device.

```python
import math
import jax
import jax.numpy as jnp
from jax import lax

D = 1024
MEMORY_HEADS = 8
HD = 128
FF = 2816
SEG = 1024
PERSIST = 16
CONV = 4
SEGMENT_TOTAL = 64
TOKENS = 65536
TGROUPS = 4


def segment_tables(key):
    base = jax.random.fold_in(key, 11)
    key_coin, key_place, key_fill = jax.random.split(base, 3)
    longest = SEGMENT_TOTAL // 2
    index = jnp.arange(SEGMENT_TOTAL, dtype=jnp.int32)
    coin = jax.random.randint(key_coin, (SEGMENT_TOTAL,), 0, 10) < 3
    begins = coin | (index % longest == 0)
    anchor = jax.random.randint(key_place, (), 0, SEGMENT_TOTAL - longest + 1)
    inside = (index > anchor) & (index < anchor + longest)
    begins = jnp.where(inside, False, begins) | (index == anchor) | (index == anchor + longest)
    starts = begins.astype(jnp.int32)
    follows = jnp.concatenate([starts[1:], jnp.ones((1,), jnp.int32)])
    partial_len = jax.random.randint(key_fill, (SEGMENT_TOTAL,), 1, SEG + 1)
    lengths = jnp.where(follows == 1, partial_len, SEG).astype(jnp.int32)
    return (starts, lengths)


def draw_seg_start(key, part):
    return segment_tables(key)[0]


def draw_seg_len(key, part):
    return segment_tables(key)[1]


def draw_memory_rates(key, part):
    key_rows = jax.random.split(jax.random.fold_in(key, 23), 9)
    fast_share = 0.5
    slow_low = 0.003
    slow_high = 0.015
    theta = jnp.exp(jax.random.uniform(key_rows[7], (SEGMENT_TOTAL, MEMORY_HEADS), jnp.float32, math.log(0.002), math.log(0.01)))
    fast = jax.random.uniform(key_rows[0], (MEMORY_HEADS,)) < fast_share
    fast_rate = jnp.exp(jax.random.uniform(key_rows[1], (MEMORY_HEADS,), jnp.float32, math.log(0.25), math.log(0.55)))
    slow_rate = jnp.exp(jax.random.uniform(key_rows[2], (MEMORY_HEADS,), jnp.float32, math.log(slow_low), math.log(slow_high)))
    baseline_rate = jnp.where(fast, fast_rate, slow_rate)
    random_noise = jnp.exp(jax.random.uniform(key_rows[3], (SEGMENT_TOTAL, MEMORY_HEADS), jnp.float32, math.log(0.6), math.log(1.6)))
    compelled_flag = jax.random.randint(key_rows[8], (), 0, SEGMENT_TOTAL)
    spike_event = (jax.random.uniform(key_rows[4], (SEGMENT_TOTAL, 1)) < 0.06) | (jnp.arange(SEGMENT_TOTAL)[:, None] == compelled_flag)
    spike_rate = jax.random.uniform(key_rows[5], (SEGMENT_TOTAL, MEMORY_HEADS), jnp.float32, 0.2, 0.5)
    decay_factor = jnp.where(spike_event, jnp.maximum(baseline_rate * random_noise, spike_rate), baseline_rate * random_noise)
    eta = jax.random.uniform(key_rows[6], (SEGMENT_TOTAL, MEMORY_HEADS), jnp.float32, 0.3, 0.8)
    return jnp.stack([decay_factor, eta, theta]).astype(jnp.float32)


def levels(rng, dims, cuts, least, top_value):
    def one(dim, shards_of):
        steps = jax.random.uniform(jax.random.fold_in(jax.random.fold_in(rng, 6), dim), (shards_of,), jnp.float32, least / len(cuts), top_value / len(cuts))
        return jnp.repeat(jnp.exp(steps), dims[dim] // shards_of).reshape((-1,) + (1,) * (len(dims) - dim - 1))

    factor_of = one(*cuts[0])
    for cut in cuts[1:]:
        factor_of = factor_of * one(*cut)
    return factor_of


def noise(stream_key, shape, scale, most, shards=(), kind=jnp.bfloat16):
    entries = scale * jax.random.normal(stream_key, shape, jnp.float32)
    if shards:
        entries = entries * levels(stream_key, shape, shards, -0.22, 0.18)
    return jnp.clip(entries, -most, most).astype(kind)


def setup_inputs(seed: int = 0) -> dict:
    arg_keys = jax.random.split(jax.random.key(seed), 12)
    return {
        "activations": noise(arg_keys[0], (TOKENS, D), 1.0, 6.0, ((0, 64), (1, 4))),
        "seg_len": draw_seg_len(jax.random.fold_in(arg_keys[11], 71), 0),
        "seg_start": draw_seg_start(jax.random.fold_in(arg_keys[11], 71), 0),
        "memory_rates": draw_memory_rates(jax.random.fold_in(arg_keys[11], 71), 0),
        "w_qkv": noise(arg_keys[4], (D, 3, MEMORY_HEADS * HD), D ** -0.5, 0.1875, ((2, 4),)),
        "conv_w": noise(arg_keys[5], (CONV, 3, MEMORY_HEADS * HD), 0.5, 3.0, ((2, 4),), jnp.float32),
        "persistent": noise(arg_keys[6], (2, PERSIST, MEMORY_HEADS * HD), 1.0, 6.0, ((2, 4),)),
        "w_out": noise(arg_keys[7], (MEMORY_HEADS * HD, D), (MEMORY_HEADS * HD) ** -0.5, 0.1875, ((0, 4),)),
        "w_gate": noise(arg_keys[8], (D, FF), D ** -0.5, 0.1875, ((1, 4),)),
        "w_up": noise(arg_keys[9], (D, FF), D ** -0.5, 0.1875, ((1, 4),)),
        "w_down": noise(arg_keys[10], (FF, D), FF ** -0.5, 0.109375, ((0, 4),)),
    }


epsilon = 1e-06
score_scale = 8.0

def unit_rows(values_in):
    return values_in * lax.rsqrt(lax.optimization_barrier(jnp.sum(values_in * values_in, -1, keepdims=True)) + epsilon)

def reference(activations, seg_len, seg_start, memory_rates, w_qkv, conv_w, persistent, w_out, w_gate, w_up, w_down):
    width = MEMORY_HEADS * HD
    wide = w_qkv.reshape(D, 3 * width)
    taps = conv_w.reshape(CONV, 3 * width).astype(jnp.float32)
    position = jnp.arange(SEG, dtype=jnp.int32)
    x_segs = activations.reshape(SEGMENT_TOTAL, SEG, D)

    def project(x_seg):
        xf = x_seg.astype(jnp.float32)
        inv_rms = lax.rsqrt(lax.optimization_barrier(jnp.sum(xf * xf, -1)) / D + epsilon)
        return (jnp.dot(x_seg, wide, preferred_element_type=jnp.float32) * inv_rms[:, None]).astype(jnp.bfloat16)
    qkv_segs = lax.map(project, x_segs)
    tails = qkv_segs[:, SEG - (CONV - 1):]
    before = jnp.concatenate([jnp.zeros((1, CONV - 1, 3 * width), jnp.bfloat16), tails[:-1]], 0)

    def convolve(inputs):
        qkv_seg, edge_rows, start_flag = inputs
        extended = jnp.concatenate([edge_rows, qkv_seg], 0)
        continuing = start_flag == 0
        total = jnp.zeros((SEG, 3 * width), jnp.float32)
        for offset in range(CONV):
            shifted = extended[CONV - 1 - offset:CONV - 1 - offset + SEG].astype(jnp.float32)
            valid = (position >= offset) | continuing
            total = total + jnp.where(valid[:, None], taps[offset] * shifted, 0.0)
        parts = total.reshape(SEG, 3, MEMORY_HEADS, HD)
        query_n = unit_rows(parts[:, 0]).astype(jnp.bfloat16)
        key_n = unit_rows(parts[:, 1]).astype(jnp.bfloat16)
        value_n = parts[:, 2].astype(jnp.bfloat16)
        return (query_n, key_n, value_n)
    qn, kn, values = lax.map(convolve, (qkv_segs, before, seg_start))
    pkeys = unit_rows(persistent[0].astype(jnp.float32).reshape(PERSIST, MEMORY_HEADS, HD)).astype(jnp.bfloat16)
    pvalues = persistent[1].reshape(PERSIST, MEMORY_HEADS, HD)
    live = position[None, :] < seg_len[:, None]
    keys_live = jnp.where(live[:, :, None, None], kn, jnp.zeros((), jnp.bfloat16))
    a_mats = jnp.einsum('cthi,cthj->chij', keys_live.astype(jnp.float32), keys_live.astype(jnp.float32))
    b_mats = jnp.einsum('cthi,cthj->chij', keys_live.astype(jnp.float32), values.astype(jnp.float32))
    rates = jnp.transpose(memory_rates, (1, 0, 2))

    def memory_step(carry, inputs):
        memory, momentum = carry
        query_seg, a_mat, b_mat, rate_row, start_flag = inputs
        keep = (1 - start_flag).astype(jnp.float32)
        memory_in = memory * keep
        momentum_in = momentum * keep
        retr = jnp.einsum('thi,hij->thj', query_seg.astype(jnp.float32), memory_in, precision=lax.Precision.HIGHEST)
        decay_factor = rate_row[0][:, None, None]
        eta = rate_row[1][:, None, None]
        theta = rate_row[2][:, None, None]
        grad = jnp.matmul(a_mat, memory_in, precision=lax.Precision.HIGHEST) - b_mat
        momentum_out = eta * momentum_in - theta * grad
        memory_out = (1.0 - decay_factor) * memory_in + momentum_out
        return ((memory_out, momentum_out), retr)
    zero_state = jnp.zeros((MEMORY_HEADS, HD, HD), jnp.float32)
    _, retr = lax.scan(memory_step, (zero_state, zero_state), (qn, a_mats, b_mats, rates, seg_start))
    mem = retr * lax.rsqrt(lax.optimization_barrier(jnp.mean(retr * retr, -1, keepdims=True)) + epsilon)

    def attend(inputs):
        query_seg, key_seg, value_seg, length = inputs
        keys_all = jnp.concatenate([pkeys, key_seg], 0).astype(jnp.float32)
        values_all = jnp.concatenate([pvalues, value_seg], 0).astype(jnp.float32)
        scores = score_scale * jnp.einsum('qhd,khd->hqk', query_seg.astype(jnp.float32), keys_all)
        rows_q = position[:, None]
        cols_k = jnp.arange(PERSIST + SEG, dtype=jnp.int32)[None, :] - PERSIST
        allow = (cols_k < 0) | (cols_k <= rows_q) & (cols_k < length)
        weights = jnp.where(allow[None], jnp.exp(scores), 0.0)
        probs = (weights / lax.optimization_barrier(jnp.sum(weights, -1, keepdims=True))).astype(jnp.bfloat16)
        return jnp.einsum('hqk,khd->qhd', probs.astype(jnp.float32), values_all)
    attn = lax.map(attend, (qn, kn, values, seg_len))
    heads_out = (attn + mem).astype(jnp.bfloat16).reshape(SEGMENT_TOTAL, SEG, width)
    group_heads = width // TGROUPS
    group_units = FF // TGROUPS

    def finish(inputs):
        x_seg, out_seg = inputs
        proj = jnp.zeros((SEG, D), jnp.float32)
        for group in range(TGROUPS):
            term = jnp.dot(out_seg[:, group * group_heads:(group + 1) * group_heads], w_out[group * group_heads:(group + 1) * group_heads], preferred_element_type=jnp.float32).astype(jnp.bfloat16)
            term = lax.optimization_barrier(term)
            proj = proj + term.astype(jnp.float32)
        resid = (x_seg.astype(jnp.float32) + proj).astype(jnp.bfloat16)
        resid_f = resid.astype(jnp.float32)
        inv_rms2 = lax.rsqrt(lax.optimization_barrier(jnp.sum(resid_f * resid_f, -1)) / D + epsilon)
        gate = jnp.dot(resid, w_gate, preferred_element_type=jnp.float32) * inv_rms2[:, None]
        up = jnp.dot(resid, w_up, preferred_element_type=jnp.float32) * inv_rms2[:, None]
        hidden = (jax.nn.silu(gate) * up).astype(jnp.bfloat16)
        ffn = jnp.zeros((SEG, D), jnp.float32)
        for group in range(TGROUPS):
            term = jnp.dot(hidden[:, group * group_units:(group + 1) * group_units], w_down[group * group_units:(group + 1) * group_units], preferred_element_type=jnp.float32).astype(jnp.bfloat16)
            term = lax.optimization_barrier(term)
            ffn = ffn + term.astype(jnp.float32)
        return (resid_f + ffn).astype(jnp.bfloat16)
    layer_out = lax.map(finish, (x_segs, heads_out))
    return layer_out.reshape(TOKENS, D)
```

```python
import jax
import jax.numpy as jnp
from jax import lax
from jax.sharding import PartitionSpec as P

HD = 128
SEG = 1024
CONV = 4
PROMPT_SPAN = 32


epsilon = 1e-06
score_scale = 8.0


def passed_along(block, axis, distance):
    devices = range(lax.axis_size(axis))
    route = [(i - distance, i) for i in devices if i - distance in devices]
    return lax.ppermute(block, axis, route)


def passed_exact(block, axis, distance):
    high = block.astype(jnp.bfloat16)
    low = (block - high.astype(jnp.float32)).astype(jnp.bfloat16)
    high, low = passed_along((high, low), axis, distance)
    return high.astype(jnp.float32) + low.astype(jnp.float32)


def window_scan(seg_map, seg_shift, axis, reach):
    distance = 1
    while distance < reach:
        if 2 * distance >= reach:
            shift_before = passed_exact(seg_shift, axis, distance)
            seg_shift = exact_product(seg_map, shift_before) + seg_shift
        else:
            high = seg_shift.astype(jnp.bfloat16)
            low = (seg_shift - high.astype(jnp.float32)).astype(jnp.bfloat16)
            map_before, high, low = passed_along(
                (seg_map.astype(jnp.bfloat16), high, low), axis, distance
            )
            shift_before = high.astype(jnp.float32) + low.astype(jnp.float32)
            seg_shift = exact_product(seg_map, shift_before) + seg_shift
            seg_map = exact_product(seg_map, map_before.astype(jnp.float32))
        distance *= 2
    return seg_shift


def unit_rows(values_in):
    return values_in * lax.rsqrt(jnp.sum(values_in * values_in, -1, keepdims=True) + epsilon)


def exact_product(left, right):
    return jnp.matmul(left, right, precision=lax.Precision.HIGHEST)


def body(
    activations,
    seg_len,
    seg_start,
    memory_rates,
    w_qkv,
    conv_w,
    persistent,
    w_out,
    w_gate,
    w_up,
    w_down,
):
    token_rows, local_feat = activations.shape
    seg_count = seg_len.shape[0]
    full_width = w_qkv.shape[0]
    head_width = w_qkv.shape[2]
    local_heads = head_width // HD
    group_index = lax.axis_index(("tr", "tc"))
    wide = w_qkv.reshape(full_width, 3 * head_width)
    row_ids = jnp.arange(token_rows, dtype=jnp.int32)
    position = row_ids % SEG
    segment_of = row_ids // SEG
    continuing = seg_start[segment_of] == 0
    piece = lax.all_gather(activations, ("tr", "tc"), axis=1, tiled=True)
    piece_f = piece.astype(jnp.float32)
    projected = jnp.dot(piece, wide, preferred_element_type=jnp.float32)
    squares = jnp.sum(piece_f * piece_f, -1)
    qkv = (projected * lax.rsqrt(squares / full_width + epsilon)[:, None]).astype(jnp.bfloat16)
    edge_rows = passed_along(qkv[token_rows - (CONV - 1) :], "seq", 1)
    extended = jnp.concatenate([edge_rows, qkv], 0)
    taps = conv_w.reshape(CONV, 3 * head_width)
    convolved = jnp.zeros((token_rows, 3 * head_width), jnp.float32)
    for offset in range(CONV):
        shifted = extended[CONV - 1 - offset : CONV - 1 - offset + token_rows].astype(jnp.float32)
        valid = (position >= offset) | continuing
        convolved = convolved + jnp.where(valid[:, None], taps[offset] * shifted, 0.0)
    parts = convolved.reshape(token_rows, 3, local_heads, HD)
    query_n = unit_rows(parts[:, 0]).astype(jnp.bfloat16)
    key_n = unit_rows(parts[:, 1]).astype(jnp.bfloat16)
    value_n = parts[:, 2].astype(jnp.bfloat16)
    pkeys = unit_rows(persistent[0].astype(jnp.float32).reshape(-1, local_heads, HD)).astype(
        jnp.bfloat16
    )
    pvalues = persistent[1].reshape(-1, local_heads, HD)
    persist_rows = pkeys.shape[0]
    live = position < seg_len[segment_of]
    keys_live = jnp.where(live[:, None, None], key_n, jnp.zeros((), jnp.bfloat16)).reshape(
        seg_count, SEG, local_heads, HD
    )
    value_segs = value_n.reshape(seg_count, SEG, local_heads, HD)
    a_mats = jnp.einsum("cthi,cthj->chij", keys_live, keys_live, preferred_element_type=jnp.float32)
    b_mats = jnp.einsum(
        "cthi,cthj->chij", keys_live, value_segs, preferred_element_type=jnp.float32
    )
    my_rates = lax.dynamic_slice_in_dim(memory_rates, group_index * local_heads, local_heads, 2)
    decay_factor = my_rates[0][:, :, None, None]
    eta = my_rates[1][:, :, None, None]
    theta = my_rates[2][:, :, None, None]
    keep = (1 - seg_start).astype(jnp.float32)[:, None, None, None]
    identity = jnp.eye(HD, dtype=jnp.float32)
    upper = jnp.concatenate([(1.0 - decay_factor) * identity - theta * a_mats, eta * identity], -1)
    lower = jnp.concatenate([-theta * a_mats, eta * identity], -1)
    seg_maps = jnp.concatenate([upper, lower], -2) * keep
    seg_shifts = jnp.concatenate([theta * b_mats, theta * b_mats], -2)
    reach = min(PROMPT_SPAN, lax.axis_size("seq"))
    state_out = window_scan(seg_maps[0], seg_shifts[0], "seq", reach)
    memory_in = passed_exact(state_out[:, :HD], "seq", 1) * keep[0]
    query_seg = query_n.astype(jnp.float32)
    retr_parts = jnp.einsum("thi,hij->thj", query_seg, memory_in, precision=lax.Precision.HIGHEST)
    mem = retr_parts * lax.rsqrt(jnp.mean(retr_parts * retr_parts, -1, keepdims=True) + epsilon)
    block_rows = min(512, SEG)
    attn_parts = []
    seg_index = 0
    first = seg_index * SEG
    keys_all = jnp.concatenate([pkeys, key_n], 0)
    values_all = jnp.concatenate([pvalues, value_n], 0)
    cols_k = jnp.arange(persist_rows + SEG, dtype=jnp.int32)[None, :] - persist_rows
    for block_start in range(0, SEG, block_rows):
        query_blk = query_n[first + block_start : first + block_start + block_rows]
        scores = score_scale * jnp.einsum(
            "qhd,khd->hqk", query_blk, keys_all, preferred_element_type=jnp.float32
        )
        rows_q = block_start + jnp.arange(block_rows, dtype=jnp.int32)[:, None]
        allow = (cols_k < 0) | (cols_k <= rows_q) & (cols_k < seg_len[seg_index])
        weights = jnp.where(allow[None], jnp.exp(scores), 0.0)
        probs = (weights / jnp.sum(weights, -1, keepdims=True)).astype(jnp.bfloat16)
        attn_parts.append(
            jnp.einsum("hqk,khd->qhd", probs, values_all, preferred_element_type=jnp.float32)
        )
    attn = jnp.concatenate(attn_parts, 0)
    heads_out = (attn + mem).astype(jnp.bfloat16).reshape(token_rows, head_width)
    partial_value = jnp.dot(heads_out, w_out, preferred_element_type=jnp.float32)
    share = lax.psum_scatter(
        partial_value.astype(jnp.bfloat16), ("tr", "tc"), scatter_dimension=1, tiled=True
    ).astype(jnp.float32)
    resid = (activations.astype(jnp.float32) + share).astype(jnp.bfloat16)
    piece = lax.all_gather(resid, ("tr", "tc"), axis=1, tiled=True)
    piece_f = piece.astype(jnp.float32)
    gate = jnp.dot(piece, w_gate, preferred_element_type=jnp.float32)
    up_proj = jnp.dot(piece, w_up, preferred_element_type=jnp.float32)
    squares2 = jnp.sum(piece_f * piece_f, -1)
    inv_rms2 = lax.rsqrt(squares2 / full_width + epsilon)[:, None]
    hidden = (jax.nn.silu(gate * inv_rms2) * (up_proj * inv_rms2)).astype(jnp.bfloat16)
    down = jnp.dot(hidden, w_down, preferred_element_type=jnp.float32)
    ffn_share = lax.psum_scatter(
        down.astype(jnp.bfloat16), ("tr", "tc"), scatter_dimension=1, tiled=True
    ).astype(jnp.float32)
    return (resid.astype(jnp.float32) + ffn_share).astype(jnp.bfloat16)


def solution(mesh):
    return jax.shard_map(
        body,
        mesh=mesh,
        in_specs=(
            P("seq", ("tr", "tc")),
            P("seq"),
            P("seq"),
            P(None, "seq", None),
            P(None, None, ("tr", "tc")),
            P(None, None, ("tr", "tc")),
            P(None, None, ("tr", "tc")),
            P(("tr", "tc"), None),
            P(None, ("tr", "tc")),
            P(None, ("tr", "tc")),
            P(("tr", "tc"), None),
        ),
        out_specs=P("seq", ("tr", "tc")),
        check_vma=False,
    )
```

```python
import jax
import jax.numpy as jnp
from jax import lax
from jax.sharding import PartitionSpec as P

HD = 128
SEG = 1024
CONV = 4
PROMPT_SPAN = 32


epsilon = 1e-06
score_scale = 8.0


def passed_along(block, axis, distance):
    devices = range(lax.axis_size(axis))
    route = [(i - distance, i) for i in devices if i - distance in devices]
    return lax.ppermute(block, axis, route)


def passed_exact(block, axis, distance):
    high = block.astype(jnp.bfloat16)
    low = (block - high.astype(jnp.float32)).astype(jnp.bfloat16)
    high, low = passed_along((high, low), axis, distance)
    return high.astype(jnp.float32) + low.astype(jnp.float32)


def window_scan(seg_map, seg_shift, axis, reach):
    distance = 1
    while distance < reach:
        if 2 * distance >= reach:
            shift_before = passed_exact(seg_shift, axis, distance)
            seg_shift = exact_product(seg_map, shift_before) + seg_shift
        else:
            high = seg_shift.astype(jnp.bfloat16)
            low = (seg_shift - high.astype(jnp.float32)).astype(jnp.bfloat16)
            map_before, high, low = passed_along(
                (seg_map.astype(jnp.bfloat16), high, low), axis, distance
            )
            shift_before = high.astype(jnp.float32) + low.astype(jnp.float32)
            seg_shift = exact_product(seg_map, shift_before) + seg_shift
            seg_map = exact_product(seg_map, map_before.astype(jnp.float32))
        distance *= 2
    return seg_shift


def group_route(axis, distance):
    count = lax.axis_size(axis)
    return [(i, (i + distance) % count) for i in range(count)]


def gathered_products(local, weights, axis):
    count, index = (lax.axis_size(axis), lax.axis_index(axis))
    width = local.shape[1]
    pieces = [(local, index)]
    for distance in range(1, count):
        arrived = lax.ppermute(local, axis, group_route(axis, distance))
        pieces.append((arrived, (index - distance) % count))
    totals = [None] * len(weights)
    squares = None
    for piece, source in pieces:
        piece_f = piece.astype(jnp.float32)
        part_sq = jnp.sum(piece_f * piece_f, -1)
        squares = part_sq if squares is None else squares + part_sq
        for k, weight in enumerate(weights):
            rows = lax.dynamic_slice_in_dim(weight, source * width, width, 0)
            term = jnp.dot(piece, rows, preferred_element_type=jnp.float32)
            totals[k] = term if totals[k] is None else totals[k] + term
    return totals, squares


def scattered_sum(left, weight, axis):
    count, index = (lax.axis_size(axis), lax.axis_index(axis))
    width = weight.shape[1] // count

    def block(owner):
        cols = lax.dynamic_slice_in_dim(weight, owner * width, width, 1)
        return jnp.dot(left, cols, preferred_element_type=jnp.float32).astype(jnp.bfloat16)

    total = None
    for distance in range(1, count):
        arrived = lax.ppermute(block((index + distance) % count), axis, group_route(axis, distance))
        total = arrived.astype(jnp.float32) if total is None else total + arrived.astype(jnp.float32)
    own = block(index).astype(jnp.float32)
    return own if total is None else total + own


def unit_rows(values_in):
    return values_in * lax.rsqrt(jnp.sum(values_in * values_in, -1, keepdims=True) + epsilon)


def exact_product(left, right):
    return jnp.matmul(left, right, precision=lax.Precision.HIGHEST)


def body(
    activations,
    seg_len,
    seg_start,
    memory_rates,
    w_qkv,
    conv_w,
    persistent,
    w_out,
    w_gate,
    w_up,
    w_down,
):
    token_rows, local_feat = activations.shape
    seg_count = seg_len.shape[0]
    full_width = w_qkv.shape[0]
    head_width = w_qkv.shape[2]
    local_heads = head_width // HD
    group_index = lax.axis_index(("tr", "tc"))
    wide = w_qkv.reshape(full_width, 3 * head_width)
    row_ids = jnp.arange(token_rows, dtype=jnp.int32)
    position = row_ids % SEG
    segment_of = row_ids // SEG
    continuing = seg_start[segment_of] == 0
    (projected,), squares = gathered_products(activations, (wide,), ("tr", "tc"))
    qkv = (projected * lax.rsqrt(squares / full_width + epsilon)[:, None]).astype(jnp.bfloat16)
    edge_rows = passed_along(qkv[token_rows - (CONV - 1) :], "seq", 1)
    extended = jnp.concatenate([edge_rows, qkv], 0)
    taps = conv_w.reshape(CONV, 3 * head_width)
    convolved = jnp.zeros((token_rows, 3 * head_width), jnp.float32)
    for offset in range(CONV):
        shifted = extended[CONV - 1 - offset : CONV - 1 - offset + token_rows].astype(jnp.float32)
        valid = (position >= offset) | continuing
        convolved = convolved + jnp.where(valid[:, None], taps[offset] * shifted, 0.0)
    parts = convolved.reshape(token_rows, 3, local_heads, HD)
    query_n = unit_rows(parts[:, 0]).astype(jnp.bfloat16)
    key_n = unit_rows(parts[:, 1]).astype(jnp.bfloat16)
    value_n = parts[:, 2].astype(jnp.bfloat16)
    pkeys = unit_rows(persistent[0].astype(jnp.float32).reshape(-1, local_heads, HD)).astype(
        jnp.bfloat16
    )
    pvalues = persistent[1].reshape(-1, local_heads, HD)
    persist_rows = pkeys.shape[0]
    live = position < seg_len[segment_of]
    keys_live = jnp.where(live[:, None, None], key_n, jnp.zeros((), jnp.bfloat16)).reshape(
        seg_count, SEG, local_heads, HD
    )
    value_segs = value_n.reshape(seg_count, SEG, local_heads, HD)
    a_mats = jnp.einsum("cthi,cthj->chij", keys_live, keys_live, preferred_element_type=jnp.float32)
    b_mats = jnp.einsum(
        "cthi,cthj->chij", keys_live, value_segs, preferred_element_type=jnp.float32
    )
    my_rates = lax.dynamic_slice_in_dim(memory_rates, group_index * local_heads, local_heads, 2)
    decay_factor = my_rates[0][:, :, None, None]
    eta = my_rates[1][:, :, None, None]
    theta = my_rates[2][:, :, None, None]
    keep = (1 - seg_start).astype(jnp.float32)[:, None, None, None]
    identity = jnp.eye(HD, dtype=jnp.float32)
    upper = jnp.concatenate([(1.0 - decay_factor) * identity - theta * a_mats, eta * identity], -1)
    lower = jnp.concatenate([-theta * a_mats, eta * identity], -1)
    seg_maps = jnp.concatenate([upper, lower], -2) * keep
    seg_shifts = jnp.concatenate([theta * b_mats, theta * b_mats], -2)
    reach = min(PROMPT_SPAN, lax.axis_size("seq"))
    state_out = window_scan(seg_maps[0], seg_shifts[0], "seq", reach)
    memory_in = passed_exact(state_out[:, :HD], "seq", 1) * keep[0]
    query_seg = query_n.astype(jnp.float32)
    retr_parts = jnp.einsum("thi,hij->thj", query_seg, memory_in, precision=lax.Precision.HIGHEST)
    mem = retr_parts * lax.rsqrt(jnp.mean(retr_parts * retr_parts, -1, keepdims=True) + epsilon)
    block_rows = min(512, SEG)
    attn_parts = []
    seg_index = 0
    first = seg_index * SEG
    keys_all = jnp.concatenate([pkeys, key_n], 0)
    values_all = jnp.concatenate([pvalues, value_n], 0)
    cols_k = jnp.arange(persist_rows + SEG, dtype=jnp.int32)[None, :] - persist_rows
    for block_start in range(0, SEG, block_rows):
        query_blk = query_n[first + block_start : first + block_start + block_rows]
        scores = score_scale * jnp.einsum(
            "qhd,khd->hqk", query_blk, keys_all, preferred_element_type=jnp.float32
        )
        rows_q = block_start + jnp.arange(block_rows, dtype=jnp.int32)[:, None]
        allow = (cols_k < 0) | (cols_k <= rows_q) & (cols_k < seg_len[seg_index])
        weights = jnp.where(allow[None], jnp.exp(scores), 0.0)
        probs = (weights / jnp.sum(weights, -1, keepdims=True)).astype(jnp.bfloat16)
        attn_parts.append(
            jnp.einsum("hqk,khd->qhd", probs, values_all, preferred_element_type=jnp.float32)
        )
    attn = jnp.concatenate(attn_parts, 0)
    heads_out = (attn + mem).astype(jnp.bfloat16).reshape(token_rows, head_width)
    share = scattered_sum(heads_out, w_out, ("tr", "tc"))
    resid = (activations.astype(jnp.float32) + share).astype(jnp.bfloat16)
    (gate, up_proj), squares2 = gathered_products(resid, (w_gate, w_up), ("tr", "tc"))
    inv_rms2 = lax.rsqrt(squares2 / full_width + epsilon)[:, None]
    hidden = (jax.nn.silu(gate * inv_rms2) * (up_proj * inv_rms2)).astype(jnp.bfloat16)
    ffn_share = scattered_sum(hidden, w_down, ("tr", "tc"))
    return (resid.astype(jnp.float32) + ffn_share).astype(jnp.bfloat16)


def solution(mesh):
    return jax.shard_map(
        body,
        mesh=mesh,
        in_specs=(
            P("seq", ("tr", "tc")),
            P("seq"),
            P("seq"),
            P(None, "seq", None),
            P(None, None, ("tr", "tc")),
            P(None, None, ("tr", "tc")),
            P(None, None, ("tr", "tc")),
            P(("tr", "tc"), None),
            P(None, ("tr", "tc")),
            P(None, ("tr", "tc")),
            P(("tr", "tc"), None),
        ),
        out_specs=P("seq", ("tr", "tc")),
        check_vma=False,
    )
```

```python
import jax
import jax.numpy as jnp
from jax import lax
from jax.sharding import PartitionSpec as P

HD = 128
SEG = 1024
CONV = 4
PROMPT_SPAN = 32


epsilon = 1e-06
score_scale = 8.0


def passed_along(block, axis, distance):
    devices = range(lax.axis_size(axis))
    route = [(i - distance, i) for i in devices if i - distance in devices]
    return lax.ppermute(block, axis, route)


def exact_pair(block):
    high = block.astype(jnp.bfloat16)
    low = (block - high.astype(jnp.float32)).astype(jnp.bfloat16)
    return jnp.concatenate([high, low], -1)


def from_pair(pair):
    half = pair.shape[-1] // 2
    return pair[..., :half].astype(jnp.float32) + pair[..., half:].astype(jnp.float32)


def memory_entering(seg_map, seg_shift, axis, reach):
    if reach < 2:
        return jnp.zeros_like(seg_shift[:, : seg_shift.shape[-1]])
    distance = 1
    while 2 * distance < reach:
        payload = jnp.concatenate([seg_map.astype(jnp.bfloat16), exact_pair(seg_shift)], -1)
        arrived = passed_along(payload, axis, distance)
        width = seg_map.shape[-1]
        shift_before = from_pair(arrived[..., width:])
        map_before = arrived[..., :width].astype(jnp.float32)
        seg_shift = exact_product(seg_map, shift_before) + seg_shift
        seg_map = exact_product(seg_map, map_before)
        distance *= 2
    rows = seg_shift.shape[-1]
    last = jnp.concatenate(
        [seg_map[:, :rows].astype(jnp.bfloat16), exact_pair(seg_shift[:, :rows])], -1
    )
    last = passed_along(last, axis, 1)
    width = seg_map.shape[-1]
    earlier = from_pair(passed_along(exact_pair(seg_shift), axis, distance + 1))
    near_map = last[..., :width].astype(jnp.float32)
    return exact_product(near_map, earlier) + from_pair(last[..., width:])


def group_route(axis, distance):
    count = lax.axis_size(axis)
    return [(i, (i + distance) % count) for i in range(count)]


def gathered_products(local, weights, axis):
    count, index = (lax.axis_size(axis), lax.axis_index(axis))
    width = local.shape[1]
    pieces = [(local, index)]
    for distance in range(1, count):
        arrived = lax.ppermute(local, axis, group_route(axis, distance))
        pieces.append((arrived, (index - distance) % count))
    totals = [None] * len(weights)
    squares = None
    for piece, source in pieces:
        piece_f = piece.astype(jnp.float32)
        part_sq = jnp.sum(piece_f * piece_f, -1)
        squares = part_sq if squares is None else squares + part_sq
        for k, weight in enumerate(weights):
            rows = lax.dynamic_slice_in_dim(weight, source * width, width, 0)
            term = jnp.dot(piece, rows, preferred_element_type=jnp.float32)
            totals[k] = term if totals[k] is None else totals[k] + term
    return totals, squares


def scattered_sum(left, weight, axis):
    count, index = (lax.axis_size(axis), lax.axis_index(axis))
    width = weight.shape[1] // count

    def block(owner):
        cols = lax.dynamic_slice_in_dim(weight, owner * width, width, 1)
        return jnp.dot(left, cols, preferred_element_type=jnp.float32).astype(jnp.bfloat16)

    total = None
    for distance in range(1, count):
        arrived = lax.ppermute(block((index + distance) % count), axis, group_route(axis, distance))
        total = arrived.astype(jnp.float32) if total is None else total + arrived.astype(jnp.float32)
    own = block(index).astype(jnp.float32)
    return own if total is None else total + own


def unit_rows(values_in):
    return values_in * lax.rsqrt(jnp.sum(values_in * values_in, -1, keepdims=True) + epsilon)


def exact_product(left, right):
    return jnp.matmul(left, right, precision=lax.Precision.HIGHEST)


def body(
    activations,
    seg_len,
    seg_start,
    memory_rates,
    w_qkv,
    conv_w,
    persistent,
    w_out,
    w_gate,
    w_up,
    w_down,
):
    token_rows, local_feat = activations.shape
    seg_count = seg_len.shape[0]
    full_width = w_qkv.shape[0]
    head_width = w_qkv.shape[2]
    local_heads = head_width // HD
    group_index = lax.axis_index(("tr", "tc"))
    wide = w_qkv.reshape(full_width, 3 * head_width)
    row_ids = jnp.arange(token_rows, dtype=jnp.int32)
    position = row_ids % SEG
    segment_of = row_ids // SEG
    continuing = seg_start[segment_of] == 0
    (projected,), squares = gathered_products(activations, (wide,), ("tr", "tc"))
    qkv = (projected * lax.rsqrt(squares / full_width + epsilon)[:, None]).astype(jnp.bfloat16)
    edge_rows = passed_along(qkv[token_rows - (CONV - 1) :], "seq", 1)
    extended = jnp.concatenate([edge_rows, qkv], 0)
    taps = conv_w.reshape(CONV, 3 * head_width)
    convolved = jnp.zeros((token_rows, 3 * head_width), jnp.float32)
    for offset in range(CONV):
        shifted = extended[CONV - 1 - offset : CONV - 1 - offset + token_rows].astype(jnp.float32)
        valid = (position >= offset) | continuing
        convolved = convolved + jnp.where(valid[:, None], taps[offset] * shifted, 0.0)
    parts = convolved.reshape(token_rows, 3, local_heads, HD)
    query_n = unit_rows(parts[:, 0]).astype(jnp.bfloat16)
    key_n = unit_rows(parts[:, 1]).astype(jnp.bfloat16)
    value_n = parts[:, 2].astype(jnp.bfloat16)
    pkeys = unit_rows(persistent[0].astype(jnp.float32).reshape(-1, local_heads, HD)).astype(
        jnp.bfloat16
    )
    pvalues = persistent[1].reshape(-1, local_heads, HD)
    persist_rows = pkeys.shape[0]
    live = position < seg_len[segment_of]
    keys_live = jnp.where(live[:, None, None], key_n, jnp.zeros((), jnp.bfloat16)).reshape(
        seg_count, SEG, local_heads, HD
    )
    value_segs = value_n.reshape(seg_count, SEG, local_heads, HD)
    a_mats = jnp.einsum("cthi,cthj->chij", keys_live, keys_live, preferred_element_type=jnp.float32)
    b_mats = jnp.einsum(
        "cthi,cthj->chij", keys_live, value_segs, preferred_element_type=jnp.float32
    )
    my_rates = lax.dynamic_slice_in_dim(memory_rates, group_index * local_heads, local_heads, 2)
    decay_factor = my_rates[0][:, :, None, None]
    eta = my_rates[1][:, :, None, None]
    theta = my_rates[2][:, :, None, None]
    keep = (1 - seg_start).astype(jnp.float32)[:, None, None, None]
    identity = jnp.eye(HD, dtype=jnp.float32)
    upper = jnp.concatenate([(1.0 - decay_factor) * identity - theta * a_mats, eta * identity], -1)
    lower = jnp.concatenate([-theta * a_mats, eta * identity], -1)
    seg_maps = jnp.concatenate([upper, lower], -2) * keep
    seg_shifts = jnp.concatenate([theta * b_mats, theta * b_mats], -2)
    reach = min(PROMPT_SPAN, lax.axis_size("seq"))
    memory_in = memory_entering(seg_maps[0], seg_shifts[0], "seq", reach) * keep[0]
    query_seg = query_n.astype(jnp.float32)
    retr_parts = jnp.einsum("thi,hij->thj", query_seg, memory_in, precision=lax.Precision.HIGHEST)
    mem = retr_parts * lax.rsqrt(jnp.mean(retr_parts * retr_parts, -1, keepdims=True) + epsilon)
    block_rows = min(512, SEG)
    attn_parts = []
    seg_index = 0
    first = seg_index * SEG
    keys_all = jnp.concatenate([pkeys, key_n], 0)
    values_all = jnp.concatenate([pvalues, value_n], 0)
    cols_k = jnp.arange(persist_rows + SEG, dtype=jnp.int32)[None, :] - persist_rows
    for block_start in range(0, SEG, block_rows):
        query_blk = query_n[first + block_start : first + block_start + block_rows]
        scores = score_scale * jnp.einsum(
            "qhd,khd->hqk", query_blk, keys_all, preferred_element_type=jnp.float32
        )
        rows_q = block_start + jnp.arange(block_rows, dtype=jnp.int32)[:, None]
        allow = (cols_k < 0) | (cols_k <= rows_q) & (cols_k < seg_len[seg_index])
        weights = jnp.where(allow[None], jnp.exp(scores), 0.0)
        probs = (weights / jnp.sum(weights, -1, keepdims=True)).astype(jnp.bfloat16)
        attn_parts.append(
            jnp.einsum("hqk,khd->qhd", probs, values_all, preferred_element_type=jnp.float32)
        )
    attn = jnp.concatenate(attn_parts, 0)
    heads_out = (attn + mem).astype(jnp.bfloat16).reshape(token_rows, head_width)
    share = scattered_sum(heads_out, w_out, ("tr", "tc"))
    resid = (activations.astype(jnp.float32) + share).astype(jnp.bfloat16)
    (gate, up_proj), squares2 = gathered_products(resid, (w_gate, w_up), ("tr", "tc"))
    inv_rms2 = lax.rsqrt(squares2 / full_width + epsilon)[:, None]
    hidden = (jax.nn.silu(gate * inv_rms2) * (up_proj * inv_rms2)).astype(jnp.bfloat16)
    ffn_share = scattered_sum(hidden, w_down, ("tr", "tc"))
    return (resid.astype(jnp.float32) + ffn_share).astype(jnp.bfloat16)


def solution(mesh):
    return jax.shard_map(
        body,
        mesh=mesh,
        in_specs=(
            P("seq", ("tr", "tc")),
            P("seq"),
            P("seq"),
            P(None, "seq", None),
            P(None, None, ("tr", "tc")),
            P(None, None, ("tr", "tc")),
            P(None, None, ("tr", "tc")),
            P(("tr", "tc"), None),
            P(None, ("tr", "tc")),
            P(None, ("tr", "tc")),
            P(("tr", "tc"), None),
        ),
        out_specs=P("seq", ("tr", "tc")),
        check_vma=False,
    )
```

```python
import jax
import jax.numpy as jnp
from jax import lax
from jax.sharding import PartitionSpec as P

HD = 128
SEG = 1024
CONV = 4
PROMPT_SPAN = 32


epsilon = 1e-06
score_scale = 8.0


def passed_along(block, axis, distance):
    devices = range(lax.axis_size(axis))
    route = [(i - distance, i) for i in devices if i - distance in devices]
    return lax.ppermute(block, axis, route)


def exact_pair(block):
    high = block.astype(jnp.bfloat16)
    low = (block - high.astype(jnp.float32)).astype(jnp.bfloat16)
    return jnp.concatenate([high, low], -1)


def from_pair(pair):
    half = pair.shape[-1] // 2
    return pair[..., :half].astype(jnp.float32) + pair[..., half:].astype(jnp.float32)


def memory_entering(seg_map, seg_shift, axis, reach):
    if reach < 2:
        return jnp.zeros_like(seg_shift[:, : seg_shift.shape[-1]])
    distance = 1
    while 2 * distance < reach:
        payload = jnp.concatenate([seg_map.astype(jnp.bfloat16), exact_pair(seg_shift)], -1)
        arrived = passed_along(payload, axis, distance)
        width = seg_map.shape[-1]
        shift_before = from_pair(arrived[..., width:])
        map_before = arrived[..., :width].astype(jnp.float32)
        seg_shift = exact_product(seg_map, shift_before) + seg_shift
        seg_map = exact_product(seg_map, map_before)
        distance *= 2
    rows = seg_shift.shape[-1]
    last = jnp.concatenate(
        [seg_map[:, :rows].astype(jnp.bfloat16), exact_pair(seg_shift[:, :rows])], -1
    )
    last = passed_along(last, axis, 1)
    width = seg_map.shape[-1]
    earlier = from_pair(passed_along(exact_pair(seg_shift), axis, distance + 1))
    near_map = last[..., :width].astype(jnp.float32)
    return exact_product(near_map, earlier) + from_pair(last[..., width:])


def ring_place(index):
    return (index % 2) * 2 + index // 2


def ring_route(axis, step):
    count = lax.axis_size(axis)
    return [(i, ring_place((ring_place(i) + step) % count)) for i in range(count)]


def gathered_products(local, weights, axis):
    count, index = (lax.axis_size(axis), lax.axis_index(axis))
    width = local.shape[1]
    place = ring_place(index)
    half = local.shape[0] // 2
    from_left = lax.ppermute(local, axis, ring_route(axis, 1))
    from_right = lax.ppermute(local, axis, ring_route(axis, -1))
    far_top = lax.ppermute(from_left[:half], axis, ring_route(axis, 1))
    far_bottom = lax.ppermute(from_right[half:], axis, ring_route(axis, -1))
    far = jnp.concatenate([far_top, far_bottom], 0)
    pieces = [
        (local, index),
        (from_left, ring_place((place - 1) % count)),
        (from_right, ring_place((place + 1) % count)),
        (far, ring_place((place + 2) % count)),
    ]
    totals = [None] * len(weights)
    squares = None
    for piece, source in pieces:
        piece_f = piece.astype(jnp.float32)
        part_sq = jnp.sum(piece_f * piece_f, -1)
        squares = part_sq if squares is None else squares + part_sq
        for k, weight in enumerate(weights):
            rows = lax.dynamic_slice_in_dim(weight, source * width, width, 0)
            term = jnp.dot(piece, rows, preferred_element_type=jnp.float32)
            totals[k] = term if totals[k] is None else totals[k] + term
    return totals, squares


def scattered_sum(left, weight, axis):
    count, index = (lax.axis_size(axis), lax.axis_index(axis))
    width = weight.shape[1] // count
    place = ring_place(index)
    half = left.shape[0] // 2

    def block(owner_place, rows=slice(None)):
        owner = ring_place(owner_place % count)
        cols = lax.dynamic_slice_in_dim(weight, owner * width, width, 1)
        return jnp.dot(left[rows], cols, preferred_element_type=jnp.float32)

    relay_top = lax.ppermute(
        block(place + 2, slice(0, half)).astype(jnp.bfloat16), axis, ring_route(axis, 1)
    )
    relay_bottom = lax.ppermute(
        block(place + 2, slice(half, None)).astype(jnp.bfloat16), axis, ring_route(axis, -1)
    )
    right_block = block(place + 1).astype(jnp.bfloat16).astype(jnp.float32)
    right_block = jnp.concatenate(
        [right_block[:half] + relay_top.astype(jnp.float32), right_block[half:]], 0
    )
    left_block = block(place - 1).astype(jnp.bfloat16).astype(jnp.float32)
    left_block = jnp.concatenate(
        [left_block[:half], left_block[half:] + relay_bottom.astype(jnp.float32)], 0
    )
    from_left = lax.ppermute(right_block.astype(jnp.bfloat16), axis, ring_route(axis, 1))
    from_right = lax.ppermute(left_block.astype(jnp.bfloat16), axis, ring_route(axis, -1))
    own = block(place).astype(jnp.bfloat16).astype(jnp.float32)
    return own + from_left.astype(jnp.float32) + from_right.astype(jnp.float32)


def unit_rows(values_in):
    return values_in * lax.rsqrt(jnp.sum(values_in * values_in, -1, keepdims=True) + epsilon)


def exact_product(left, right):
    return jnp.matmul(left, right, precision=lax.Precision.HIGHEST)


def body(
    activations,
    seg_len,
    seg_start,
    memory_rates,
    w_qkv,
    conv_w,
    persistent,
    w_out,
    w_gate,
    w_up,
    w_down,
):
    token_rows, local_feat = activations.shape
    seg_count = seg_len.shape[0]
    full_width = w_qkv.shape[0]
    head_width = w_qkv.shape[2]
    local_heads = head_width // HD
    group_index = lax.axis_index(("tr", "tc"))
    wide = w_qkv.reshape(full_width, 3 * head_width)
    row_ids = jnp.arange(token_rows, dtype=jnp.int32)
    position = row_ids % SEG
    segment_of = row_ids // SEG
    continuing = seg_start[segment_of] == 0
    (projected,), squares = gathered_products(activations, (wide,), ("tr", "tc"))
    qkv = (projected * lax.rsqrt(squares / full_width + epsilon)[:, None]).astype(jnp.bfloat16)
    edge_rows = passed_along(qkv[token_rows - (CONV - 1) :], "seq", 1)
    extended = jnp.concatenate([edge_rows, qkv], 0)
    taps = conv_w.reshape(CONV, 3 * head_width)
    convolved = jnp.zeros((token_rows, 3 * head_width), jnp.float32)
    for offset in range(CONV):
        shifted = extended[CONV - 1 - offset : CONV - 1 - offset + token_rows].astype(jnp.float32)
        valid = (position >= offset) | continuing
        convolved = convolved + jnp.where(valid[:, None], taps[offset] * shifted, 0.0)
    parts = convolved.reshape(token_rows, 3, local_heads, HD)
    query_n = unit_rows(parts[:, 0]).astype(jnp.bfloat16)
    key_n = unit_rows(parts[:, 1]).astype(jnp.bfloat16)
    value_n = parts[:, 2].astype(jnp.bfloat16)
    pkeys = unit_rows(persistent[0].astype(jnp.float32).reshape(-1, local_heads, HD)).astype(
        jnp.bfloat16
    )
    pvalues = persistent[1].reshape(-1, local_heads, HD)
    persist_rows = pkeys.shape[0]
    live = position < seg_len[segment_of]
    keys_live = jnp.where(live[:, None, None], key_n, jnp.zeros((), jnp.bfloat16)).reshape(
        seg_count, SEG, local_heads, HD
    )
    value_segs = value_n.reshape(seg_count, SEG, local_heads, HD)
    a_mats = jnp.einsum("cthi,cthj->chij", keys_live, keys_live, preferred_element_type=jnp.float32)
    b_mats = jnp.einsum(
        "cthi,cthj->chij", keys_live, value_segs, preferred_element_type=jnp.float32
    )
    my_rates = lax.dynamic_slice_in_dim(memory_rates, group_index * local_heads, local_heads, 2)
    decay_factor = my_rates[0][:, :, None, None]
    eta = my_rates[1][:, :, None, None]
    theta = my_rates[2][:, :, None, None]
    keep = (1 - seg_start).astype(jnp.float32)[:, None, None, None]
    identity = jnp.eye(HD, dtype=jnp.float32)
    upper = jnp.concatenate([(1.0 - decay_factor) * identity - theta * a_mats, eta * identity], -1)
    lower = jnp.concatenate([-theta * a_mats, eta * identity], -1)
    seg_maps = jnp.concatenate([upper, lower], -2) * keep
    seg_shifts = jnp.concatenate([theta * b_mats, theta * b_mats], -2)
    reach = min(PROMPT_SPAN, lax.axis_size("seq"))
    memory_in = memory_entering(seg_maps[0], seg_shifts[0], "seq", reach) * keep[0]
    query_seg = query_n.astype(jnp.float32)
    retr_parts = jnp.einsum("thi,hij->thj", query_seg, memory_in, precision=lax.Precision.HIGHEST)
    mem = retr_parts * lax.rsqrt(jnp.mean(retr_parts * retr_parts, -1, keepdims=True) + epsilon)
    block_rows = min(512, SEG)
    attn_parts = []
    seg_index = 0
    first = seg_index * SEG
    keys_all = jnp.concatenate([pkeys, key_n], 0)
    values_all = jnp.concatenate([pvalues, value_n], 0)
    cols_k = jnp.arange(persist_rows + SEG, dtype=jnp.int32)[None, :] - persist_rows
    for block_start in range(0, SEG, block_rows):
        query_blk = query_n[first + block_start : first + block_start + block_rows]
        scores = score_scale * jnp.einsum(
            "qhd,khd->hqk", query_blk, keys_all, preferred_element_type=jnp.float32
        )
        rows_q = block_start + jnp.arange(block_rows, dtype=jnp.int32)[:, None]
        allow = (cols_k < 0) | (cols_k <= rows_q) & (cols_k < seg_len[seg_index])
        weights = jnp.where(allow[None], jnp.exp(scores), 0.0)
        probs = (weights / jnp.sum(weights, -1, keepdims=True)).astype(jnp.bfloat16)
        attn_parts.append(
            jnp.einsum("hqk,khd->qhd", probs, values_all, preferred_element_type=jnp.float32)
        )
    attn = jnp.concatenate(attn_parts, 0)
    heads_out = (attn + mem).astype(jnp.bfloat16).reshape(token_rows, head_width)
    share = scattered_sum(heads_out, w_out, ("tr", "tc"))
    resid = (activations.astype(jnp.float32) + share).astype(jnp.bfloat16)
    (gate, up_proj), squares2 = gathered_products(resid, (w_gate, w_up), ("tr", "tc"))
    inv_rms2 = lax.rsqrt(squares2 / full_width + epsilon)[:, None]
    hidden = (jax.nn.silu(gate * inv_rms2) * (up_proj * inv_rms2)).astype(jnp.bfloat16)
    ffn_share = scattered_sum(hidden, w_down, ("tr", "tc"))
    return (resid.astype(jnp.float32) + ffn_share).astype(jnp.bfloat16)


def solution(mesh):
    return jax.shard_map(
        body,
        mesh=mesh,
        in_specs=(
            P("seq", ("tr", "tc")),
            P("seq"),
            P("seq"),
            P(None, "seq", None),
            P(None, None, ("tr", "tc")),
            P(None, None, ("tr", "tc")),
            P(None, None, ("tr", "tc")),
            P(("tr", "tc"), None),
            P(None, ("tr", "tc")),
            P(None, ("tr", "tc")),
            P(("tr", "tc"), None),
        ),
        out_specs=P("seq", ("tr", "tc")),
        check_vma=False,
    )
```

```python
import jax
import jax.numpy as jnp
from jax import lax
from jax.sharding import PartitionSpec as P

HD = 128
SEG = 1024
CONV = 4
PROMPT_SPAN = 32


epsilon = 1e-06
score_scale = 8.0


def passed_along(block, axis, distance):
    devices = range(lax.axis_size(axis))
    route = [(i - distance, i) for i in devices if i - distance in devices]
    return lax.ppermute(block, axis, route)


def exact_pair(block):
    high = block.astype(jnp.bfloat16)
    low = (block - high.astype(jnp.float32)).astype(jnp.bfloat16)
    return jnp.concatenate([high, low], -1)


def from_pair(pair):
    half = pair.shape[-1] // 2
    return pair[..., :half].astype(jnp.float32) + pair[..., half:].astype(jnp.float32)


def memory_entering(seg_map, seg_shift, axis, reach):
    if reach < 2:
        return jnp.zeros_like(seg_shift[:, : seg_shift.shape[-1]])
    distance = 1
    while 2 * distance < reach:
        payload = jnp.concatenate([seg_map, seg_shift], -1).astype(jnp.bfloat16)
        arrived = passed_along(payload, axis, distance)
        width = seg_map.shape[-1]
        shift_before = arrived[..., width:].astype(jnp.float32)
        map_before = arrived[..., :width].astype(jnp.float32)
        seg_shift = exact_product(seg_map, shift_before) + seg_shift
        seg_map = exact_product(seg_map, map_before)
        distance *= 2
    rows = seg_shift.shape[-1]
    last = jnp.concatenate(
        [seg_map[:, :rows].astype(jnp.bfloat16), exact_pair(seg_shift[:, :rows])], -1
    )
    last = passed_along(last, axis, 1)
    width = seg_map.shape[-1]
    earlier = from_pair(passed_along(exact_pair(seg_shift), axis, distance + 1))
    near_map = last[..., :width].astype(jnp.float32)
    return exact_product(near_map, earlier) + from_pair(last[..., width:])


def ring_place(index):
    return (index % 2) * 2 + index // 2


def ring_route(axis, step):
    count = lax.axis_size(axis)
    return [(i, ring_place((ring_place(i) + step) % count)) for i in range(count)]


def gathered_products(local, weights, axis):
    count, index = (lax.axis_size(axis), lax.axis_index(axis))
    width = local.shape[1]
    place = ring_place(index)
    half = local.shape[0] // 2
    from_left = lax.ppermute(local, axis, ring_route(axis, 1))
    from_right = lax.ppermute(local, axis, ring_route(axis, -1))
    far_top = lax.ppermute(from_left[:half], axis, ring_route(axis, 1))
    far_bottom = lax.ppermute(from_right[half:], axis, ring_route(axis, -1))
    far = jnp.concatenate([far_top, far_bottom], 0)
    pieces = [
        (local, index),
        (from_left, ring_place((place - 1) % count)),
        (from_right, ring_place((place + 1) % count)),
        (far, ring_place((place + 2) % count)),
    ]
    totals = [None] * len(weights)
    squares = None
    for piece, source in pieces:
        piece_f = piece.astype(jnp.float32)
        part_sq = jnp.sum(piece_f * piece_f, -1)
        squares = part_sq if squares is None else squares + part_sq
        for k, weight in enumerate(weights):
            rows = lax.dynamic_slice_in_dim(weight, source * width, width, 0)
            term = jnp.dot(piece, rows, preferred_element_type=jnp.float32)
            totals[k] = term if totals[k] is None else totals[k] + term
    return totals, squares


def direct_products(local, weights, axis):
    count, index = (lax.axis_size(axis), lax.axis_index(axis))
    width = local.shape[1]
    pieces = [(local, index)]
    for distance in range(1, count):
        route = [(i, (i + distance) % count) for i in range(count)]
        pieces.append((lax.ppermute(local, axis, route), (index - distance) % count))
    totals = [None] * len(weights)
    squares = None
    for piece, source in pieces:
        piece_f = piece.astype(jnp.float32)
        part_sq = jnp.sum(piece_f * piece_f, -1)
        squares = part_sq if squares is None else squares + part_sq
        for k, weight in enumerate(weights):
            rows = lax.dynamic_slice_in_dim(weight, source * width, width, 0)
            term = jnp.dot(piece, rows, preferred_element_type=jnp.float32)
            totals[k] = term if totals[k] is None else totals[k] + term
    return totals, squares


def scattered_sum(left, weight, axis):
    count, index = (lax.axis_size(axis), lax.axis_index(axis))
    width = weight.shape[1] // count
    place = ring_place(index)
    half = left.shape[0] // 2

    def block(owner_place, rows=slice(None)):
        owner = ring_place(owner_place % count)
        cols = lax.dynamic_slice_in_dim(weight, owner * width, width, 1)
        return jnp.dot(left[rows], cols, preferred_element_type=jnp.float32)

    relay_top = lax.ppermute(
        block(place + 2, slice(0, half)).astype(jnp.bfloat16), axis, ring_route(axis, 1)
    )
    relay_bottom = lax.ppermute(
        block(place + 2, slice(half, None)).astype(jnp.bfloat16), axis, ring_route(axis, -1)
    )
    right_block = block(place + 1).astype(jnp.bfloat16).astype(jnp.float32)
    right_block = jnp.concatenate(
        [right_block[:half] + relay_top.astype(jnp.float32), right_block[half:]], 0
    )
    left_block = block(place - 1).astype(jnp.bfloat16).astype(jnp.float32)
    left_block = jnp.concatenate(
        [left_block[:half], left_block[half:] + relay_bottom.astype(jnp.float32)], 0
    )
    from_left = lax.ppermute(right_block.astype(jnp.bfloat16), axis, ring_route(axis, 1))
    from_right = lax.ppermute(left_block.astype(jnp.bfloat16), axis, ring_route(axis, -1))
    own = block(place).astype(jnp.bfloat16).astype(jnp.float32)
    return own + from_left.astype(jnp.float32) + from_right.astype(jnp.float32)


def unit_rows(values_in):
    return values_in * lax.rsqrt(jnp.sum(values_in * values_in, -1, keepdims=True) + epsilon)


def exact_product(left, right):
    return jnp.matmul(left, right, precision=lax.Precision.HIGHEST)


def body(
    activations,
    seg_len,
    seg_start,
    memory_rates,
    w_qkv,
    conv_w,
    persistent,
    w_out,
    w_gate,
    w_up,
    w_down,
):
    token_rows, local_feat = activations.shape
    seg_count = seg_len.shape[0]
    full_width = w_qkv.shape[0]
    head_width = w_qkv.shape[2]
    local_heads = head_width // HD
    group_index = lax.axis_index(("tr", "tc"))
    wide = w_qkv.reshape(full_width, 3 * head_width)
    row_ids = jnp.arange(token_rows, dtype=jnp.int32)
    position = row_ids % SEG
    segment_of = row_ids // SEG
    continuing = seg_start[segment_of] == 0
    (projected,), squares = direct_products(activations, (wide,), ("tr", "tc"))
    qkv = (projected * lax.rsqrt(squares / full_width + epsilon)[:, None]).astype(jnp.bfloat16)
    edge_rows = passed_along(qkv[token_rows - (CONV - 1) :], "seq", 1)
    extended = jnp.concatenate([edge_rows, qkv], 0)
    taps = conv_w.reshape(CONV, 3 * head_width)
    convolved = jnp.zeros((token_rows, 3 * head_width), jnp.float32)
    for offset in range(CONV):
        shifted = extended[CONV - 1 - offset : CONV - 1 - offset + token_rows].astype(jnp.float32)
        valid = (position >= offset) | continuing
        convolved = convolved + jnp.where(valid[:, None], taps[offset] * shifted, 0.0)
    parts = convolved.reshape(token_rows, 3, local_heads, HD)
    query_n = unit_rows(parts[:, 0]).astype(jnp.bfloat16)
    key_n = unit_rows(parts[:, 1]).astype(jnp.bfloat16)
    value_n = parts[:, 2].astype(jnp.bfloat16)
    pkeys = unit_rows(persistent[0].astype(jnp.float32).reshape(-1, local_heads, HD)).astype(
        jnp.bfloat16
    )
    pvalues = persistent[1].reshape(-1, local_heads, HD)
    persist_rows = pkeys.shape[0]
    live = position < seg_len[segment_of]
    keys_live = jnp.where(live[:, None, None], key_n, jnp.zeros((), jnp.bfloat16)).reshape(
        seg_count, SEG, local_heads, HD
    )
    value_segs = value_n.reshape(seg_count, SEG, local_heads, HD)
    a_mats = jnp.einsum("cthi,cthj->chij", keys_live, keys_live, preferred_element_type=jnp.float32)
    b_mats = jnp.einsum(
        "cthi,cthj->chij", keys_live, value_segs, preferred_element_type=jnp.float32
    )
    my_rates = lax.dynamic_slice_in_dim(memory_rates, group_index * local_heads, local_heads, 2)
    decay_factor = my_rates[0][:, :, None, None]
    eta = my_rates[1][:, :, None, None]
    theta = my_rates[2][:, :, None, None]
    keep = (1 - seg_start).astype(jnp.float32)[:, None, None, None]
    identity = jnp.eye(HD, dtype=jnp.float32)
    upper = jnp.concatenate([(1.0 - decay_factor) * identity - theta * a_mats, eta * identity], -1)
    lower = jnp.concatenate([-theta * a_mats, eta * identity], -1)
    seg_maps = jnp.concatenate([upper, lower], -2) * keep
    seg_shifts = jnp.concatenate([theta * b_mats, theta * b_mats], -2)
    reach = min(PROMPT_SPAN, lax.axis_size("seq"))
    memory_in = memory_entering(seg_maps[0], seg_shifts[0], "seq", reach) * keep[0]
    query_seg = query_n.astype(jnp.float32)
    retr_parts = jnp.einsum("thi,hij->thj", query_seg, memory_in, precision=lax.Precision.HIGHEST)
    mem = retr_parts * lax.rsqrt(jnp.mean(retr_parts * retr_parts, -1, keepdims=True) + epsilon)
    block_rows = min(512, SEG)
    attn_parts = []
    seg_index = 0
    first = seg_index * SEG
    keys_all = jnp.concatenate([pkeys, key_n], 0)
    values_all = jnp.concatenate([pvalues, value_n], 0)
    cols_k = jnp.arange(persist_rows + SEG, dtype=jnp.int32)[None, :] - persist_rows
    for block_start in range(0, SEG, block_rows):
        query_blk = query_n[first + block_start : first + block_start + block_rows]
        scores = score_scale * jnp.einsum(
            "qhd,khd->hqk", query_blk, keys_all, preferred_element_type=jnp.float32
        )
        rows_q = block_start + jnp.arange(block_rows, dtype=jnp.int32)[:, None]
        allow = (cols_k < 0) | (cols_k <= rows_q) & (cols_k < seg_len[seg_index])
        weights = jnp.where(allow[None], jnp.exp(scores), 0.0)
        probs = (weights / jnp.sum(weights, -1, keepdims=True)).astype(jnp.bfloat16)
        attn_parts.append(
            jnp.einsum("hqk,khd->qhd", probs, values_all, preferred_element_type=jnp.float32)
        )
    attn = jnp.concatenate(attn_parts, 0)
    heads_out = (attn + mem).astype(jnp.bfloat16).reshape(token_rows, head_width)
    share = scattered_sum(heads_out, w_out, ("tr", "tc"))
    resid = (activations.astype(jnp.float32) + share).astype(jnp.bfloat16)
    (gate, up_proj), squares2 = gathered_products(resid, (w_gate, w_up), ("tr", "tc"))
    inv_rms2 = lax.rsqrt(squares2 / full_width + epsilon)[:, None]
    hidden = (jax.nn.silu(gate * inv_rms2) * (up_proj * inv_rms2)).astype(jnp.bfloat16)
    ffn_share = scattered_sum(hidden, w_down, ("tr", "tc"))
    return (resid.astype(jnp.float32) + ffn_share).astype(jnp.bfloat16)


def solution(mesh):
    return jax.shard_map(
        body,
        mesh=mesh,
        in_specs=(
            P("seq", ("tr", "tc")),
            P("seq"),
            P("seq"),
            P(None, "seq", None),
            P(None, None, ("tr", "tc")),
            P(None, None, ("tr", "tc")),
            P(None, None, ("tr", "tc")),
            P(("tr", "tc"), None),
            P(None, ("tr", "tc")),
            P(None, ("tr", "tc")),
            P(("tr", "tc"), None),
        ),
        out_specs=P("seq", ("tr", "tc")),
        check_vma=False,
    )
```

```python
import jax
import jax.numpy as jnp
from jax import lax
from jax.sharding import PartitionSpec as P

HD = 128
SEG = 1024
CONV = 4
PROMPT_SPAN = 32


epsilon = 1e-06
score_scale = 8.0


def passed_along(block, axis, distance):
    devices = range(lax.axis_size(axis))
    route = [(i - distance, i) for i in devices if i - distance in devices]
    return lax.ppermute(block, axis, route)


def exact_pair(block):
    high = block.astype(jnp.bfloat16)
    low = (block - high.astype(jnp.float32)).astype(jnp.bfloat16)
    return jnp.concatenate([high, low], -1)


def from_pair(pair):
    half = pair.shape[-1] // 2
    return pair[..., :half].astype(jnp.float32) + pair[..., half:].astype(jnp.float32)


def memory_entering(seg_map, seg_shift, axis, reach):
    if reach < 2:
        return jnp.zeros_like(seg_shift[:, : seg_shift.shape[-1]])
    distance = 1
    while 2 * distance < reach:
        payload = jnp.concatenate([seg_map, seg_shift], -1).astype(jnp.bfloat16)
        arrived = passed_along(payload, axis, distance)
        width = seg_map.shape[-1]
        moved = exact_product(seg_map, arrived.astype(jnp.float32))
        seg_shift = moved[..., width:] + seg_shift
        seg_map = moved[..., :width]
        distance *= 2
    rows = seg_shift.shape[-1]
    last = jnp.concatenate(
        [seg_map[:, :rows].astype(jnp.bfloat16), exact_pair(seg_shift[:, :rows])], -1
    )
    last = passed_along(last, axis, 1)
    width = seg_map.shape[-1]
    earlier = passed_along(seg_shift.astype(jnp.bfloat16), axis, distance + 1).astype(jnp.float32)
    near_map = last[..., :width].astype(jnp.float32)
    return exact_product(near_map, earlier) + from_pair(last[..., width:])


def ring_place(index):
    return (index % 2) * 2 + index // 2


def ring_route(axis, step):
    count = lax.axis_size(axis)
    return [(i, ring_place((ring_place(i) + step) % count)) for i in range(count)]


def gathered_products(local, weights, axis):
    count, index = (lax.axis_size(axis), lax.axis_index(axis))
    width = local.shape[1]
    place = ring_place(index)
    half = local.shape[0] // 2
    from_left = lax.ppermute(local, axis, ring_route(axis, 1))
    from_right = lax.ppermute(local, axis, ring_route(axis, -1))
    far_top = lax.ppermute(from_left[:half], axis, ring_route(axis, 1))
    far_bottom = lax.ppermute(from_right[half:], axis, ring_route(axis, -1))
    far = jnp.concatenate([far_top, far_bottom], 0)
    pieces = [
        (local, index),
        (from_left, ring_place((place - 1) % count)),
        (from_right, ring_place((place + 1) % count)),
        (far, ring_place((place + 2) % count)),
    ]
    totals = [None] * len(weights)
    squares = None
    for piece, source in pieces:
        piece_f = piece.astype(jnp.float32)
        part_sq = jnp.sum(piece_f * piece_f, -1)
        squares = part_sq if squares is None else squares + part_sq
        for k, weight in enumerate(weights):
            rows = lax.dynamic_slice_in_dim(weight, source * width, width, 0)
            term = jnp.dot(piece, rows, preferred_element_type=jnp.float32)
            totals[k] = term if totals[k] is None else totals[k] + term
    return totals, squares


def direct_products(local, weights, axis):
    count, index = (lax.axis_size(axis), lax.axis_index(axis))
    width = local.shape[1]
    pieces = [(local, index)]
    for distance in range(1, count):
        route = [(i, (i + distance) % count) for i in range(count)]
        pieces.append((lax.ppermute(local, axis, route), (index - distance) % count))
    totals = [None] * len(weights)
    squares = None
    for piece, source in pieces:
        piece_f = piece.astype(jnp.float32)
        part_sq = jnp.sum(piece_f * piece_f, -1)
        squares = part_sq if squares is None else squares + part_sq
        for k, weight in enumerate(weights):
            rows = lax.dynamic_slice_in_dim(weight, source * width, width, 0)
            term = jnp.dot(piece, rows, preferred_element_type=jnp.float32)
            totals[k] = term if totals[k] is None else totals[k] + term
    return totals, squares


def scattered_sum(left, weight, axis):
    count, index = (lax.axis_size(axis), lax.axis_index(axis))
    width = weight.shape[1] // count
    place = ring_place(index)
    half = left.shape[0] // 2

    def block(owner_place, rows=slice(None)):
        owner = ring_place(owner_place % count)
        cols = lax.dynamic_slice_in_dim(weight, owner * width, width, 1)
        return jnp.dot(left[rows], cols, preferred_element_type=jnp.float32)

    relay_top = lax.ppermute(
        block(place + 2, slice(0, half)).astype(jnp.bfloat16), axis, ring_route(axis, 1)
    )
    relay_bottom = lax.ppermute(
        block(place + 2, slice(half, None)).astype(jnp.bfloat16), axis, ring_route(axis, -1)
    )
    right_block = block(place + 1).astype(jnp.bfloat16).astype(jnp.float32)
    right_block = jnp.concatenate(
        [right_block[:half] + relay_top.astype(jnp.float32), right_block[half:]], 0
    )
    left_block = block(place - 1).astype(jnp.bfloat16).astype(jnp.float32)
    left_block = jnp.concatenate(
        [left_block[:half], left_block[half:] + relay_bottom.astype(jnp.float32)], 0
    )
    from_left = lax.ppermute(right_block.astype(jnp.bfloat16), axis, ring_route(axis, 1))
    from_right = lax.ppermute(left_block.astype(jnp.bfloat16), axis, ring_route(axis, -1))
    own = block(place).astype(jnp.bfloat16).astype(jnp.float32)
    return own + from_left.astype(jnp.float32) + from_right.astype(jnp.float32)


def unit_rows(values_in):
    return values_in * lax.rsqrt(jnp.sum(values_in * values_in, -1, keepdims=True) + epsilon)


def exact_product(left, right):
    return jnp.matmul(left, right, precision=lax.Precision.HIGHEST)


def body(
    activations,
    seg_len,
    seg_start,
    memory_rates,
    w_qkv,
    conv_w,
    persistent,
    w_out,
    w_gate,
    w_up,
    w_down,
):
    token_rows, local_feat = activations.shape
    seg_count = seg_len.shape[0]
    full_width = w_qkv.shape[0]
    head_width = w_qkv.shape[2]
    local_heads = head_width // HD
    group_index = lax.axis_index(("tr", "tc"))
    wide = w_qkv.reshape(full_width, 3 * head_width)
    row_ids = jnp.arange(token_rows, dtype=jnp.int32)
    position = row_ids % SEG
    segment_of = row_ids // SEG
    continuing = seg_start[segment_of] == 0
    (projected,), squares = direct_products(activations, (wide,), ("tr", "tc"))
    qkv = (projected * lax.rsqrt(squares / full_width + epsilon)[:, None]).astype(jnp.bfloat16)
    edge_rows = passed_along(qkv[token_rows - (CONV - 1) :], "seq", 1)
    extended = jnp.concatenate([edge_rows, qkv], 0)
    taps = conv_w.reshape(CONV, 3 * head_width)
    convolved = jnp.zeros((token_rows, 3 * head_width), jnp.float32)
    for offset in range(CONV):
        shifted = extended[CONV - 1 - offset : CONV - 1 - offset + token_rows].astype(jnp.float32)
        valid = (position >= offset) | continuing
        convolved = convolved + jnp.where(valid[:, None], taps[offset] * shifted, 0.0)
    parts = convolved.reshape(token_rows, 3, local_heads, HD)
    query_n = unit_rows(parts[:, 0]).astype(jnp.bfloat16)
    key_n = unit_rows(parts[:, 1]).astype(jnp.bfloat16)
    value_n = parts[:, 2].astype(jnp.bfloat16)
    pkeys = unit_rows(persistent[0].astype(jnp.float32).reshape(-1, local_heads, HD)).astype(
        jnp.bfloat16
    )
    pvalues = persistent[1].reshape(-1, local_heads, HD)
    persist_rows = pkeys.shape[0]
    live = position < seg_len[segment_of]
    keys_live = jnp.where(live[:, None, None], key_n, jnp.zeros((), jnp.bfloat16)).reshape(
        seg_count, SEG, local_heads, HD
    )
    value_segs = value_n.reshape(seg_count, SEG, local_heads, HD)
    a_mats = jnp.einsum("cthi,cthj->chij", keys_live, keys_live, preferred_element_type=jnp.float32)
    b_mats = jnp.einsum(
        "cthi,cthj->chij", keys_live, value_segs, preferred_element_type=jnp.float32
    )
    my_rates = lax.dynamic_slice_in_dim(memory_rates, group_index * local_heads, local_heads, 2)
    decay_factor = my_rates[0][:, :, None, None]
    eta = my_rates[1][:, :, None, None]
    theta = my_rates[2][:, :, None, None]
    keep = (1 - seg_start).astype(jnp.float32)[:, None, None, None]
    identity = jnp.eye(HD, dtype=jnp.float32)
    upper = jnp.concatenate([(1.0 - decay_factor) * identity - theta * a_mats, eta * identity], -1)
    lower = jnp.concatenate([-theta * a_mats, eta * identity], -1)
    seg_maps = jnp.concatenate([upper, lower], -2) * keep
    seg_shifts = jnp.concatenate([theta * b_mats, theta * b_mats], -2)
    reach = min(PROMPT_SPAN, lax.axis_size("seq"))
    memory_in = memory_entering(seg_maps[0], seg_shifts[0], "seq", reach) * keep[0]
    query_seg = query_n.astype(jnp.float32)
    retr_parts = jnp.einsum("thi,hij->thj", query_seg, memory_in, precision=lax.Precision.HIGHEST)
    mem = retr_parts * lax.rsqrt(jnp.mean(retr_parts * retr_parts, -1, keepdims=True) + epsilon)
    block_rows = min(512, SEG)
    attn_parts = []
    seg_index = 0
    first = seg_index * SEG
    keys_all = jnp.concatenate([pkeys, key_n], 0)
    values_all = jnp.concatenate([pvalues, value_n], 0)
    cols_k = jnp.arange(persist_rows + SEG, dtype=jnp.int32)[None, :] - persist_rows
    for block_start in range(0, SEG, block_rows):
        query_blk = query_n[first + block_start : first + block_start + block_rows]
        scores = score_scale * jnp.einsum(
            "qhd,khd->hqk", query_blk, keys_all, preferred_element_type=jnp.float32
        )
        rows_q = block_start + jnp.arange(block_rows, dtype=jnp.int32)[:, None]
        allow = (cols_k < 0) | (cols_k <= rows_q) & (cols_k < seg_len[seg_index])
        weights = jnp.where(allow[None], jnp.exp(scores), 0.0)
        probs = (weights / jnp.sum(weights, -1, keepdims=True)).astype(jnp.bfloat16)
        attn_parts.append(
            jnp.einsum("hqk,khd->qhd", probs, values_all, preferred_element_type=jnp.float32)
        )
    attn = jnp.concatenate(attn_parts, 0)
    heads_out = (attn + mem).astype(jnp.bfloat16).reshape(token_rows, head_width)
    share = scattered_sum(heads_out, w_out, ("tr", "tc"))
    resid = (activations.astype(jnp.float32) + share).astype(jnp.bfloat16)
    (gate, up_proj), squares2 = gathered_products(resid, (w_gate, w_up), ("tr", "tc"))
    inv_rms2 = lax.rsqrt(squares2 / full_width + epsilon)[:, None]
    hidden = (jax.nn.silu(gate * inv_rms2) * (up_proj * inv_rms2)).astype(jnp.bfloat16)
    ffn_share = scattered_sum(hidden, w_down, ("tr", "tc"))
    return (resid.astype(jnp.float32) + ffn_share).astype(jnp.bfloat16)


def solution(mesh):
    return jax.shard_map(
        body,
        mesh=mesh,
        in_specs=(
            P("seq", ("tr", "tc")),
            P("seq"),
            P("seq"),
            P(None, "seq", None),
            P(None, None, ("tr", "tc")),
            P(None, None, ("tr", "tc")),
            P(None, None, ("tr", "tc")),
            P(("tr", "tc"), None),
            P(None, ("tr", "tc")),
            P(None, ("tr", "tc")),
            P(("tr", "tc"), None),
        ),
        out_specs=P("seq", ("tr", "tc")),
        check_vma=False,
    )
```

```python
import jax
import jax.numpy as jnp
from jax import lax
from jax.sharding import PartitionSpec as P

HD = 128
SEG = 1024
CONV = 4
PROMPT_SPAN = 32
FINISH_CHUNKS = 2


epsilon = 1e-06
score_scale = 8.0


def passed_along(block, axis, distance):
    devices = range(lax.axis_size(axis))
    route = [(i - distance, i) for i in devices if i - distance in devices]
    return lax.ppermute(block, axis, route)


def exact_pair(block):
    high = block.astype(jnp.bfloat16)
    low = (block - high.astype(jnp.float32)).astype(jnp.bfloat16)
    return jnp.concatenate([high, low], -1)


def from_pair(pair):
    half = pair.shape[-1] // 2
    return pair[..., :half].astype(jnp.float32) + pair[..., half:].astype(jnp.float32)


def memory_entering(seg_map, seg_shift, axis, reach):
    if reach < 2:
        return jnp.zeros_like(seg_shift[:, : seg_shift.shape[-1]])
    distance = 1
    while 2 * distance < reach:
        payload = jnp.concatenate([seg_map, seg_shift], -1).astype(jnp.bfloat16)
        arrived = passed_along(payload, axis, distance)
        width = seg_map.shape[-1]
        moved = exact_product(seg_map, arrived.astype(jnp.float32))
        seg_shift = moved[..., width:] + seg_shift
        seg_map = moved[..., :width]
        distance *= 2
    rows = seg_shift.shape[-1]
    last = jnp.concatenate(
        [seg_map[:, :rows].astype(jnp.bfloat16), exact_pair(seg_shift[:, :rows])], -1
    )
    last = passed_along(last, axis, 1)
    width = seg_map.shape[-1]
    earlier = passed_along(seg_shift.astype(jnp.bfloat16), axis, distance + 1).astype(jnp.float32)
    near_map = last[..., :width].astype(jnp.float32)
    return exact_product(near_map, earlier) + from_pair(last[..., width:])


def ring_place(index):
    return (index % 2) * 2 + index // 2


def ring_route(axis, step):
    count = lax.axis_size(axis)
    return [(i, ring_place((ring_place(i) + step) % count)) for i in range(count)]


def gathered_products(local, weights, axis):
    count, index = (lax.axis_size(axis), lax.axis_index(axis))
    width = local.shape[1]
    place = ring_place(index)
    half = local.shape[0] // 2
    from_left = lax.ppermute(local, axis, ring_route(axis, 1))
    from_right = lax.ppermute(local, axis, ring_route(axis, -1))
    far_top = lax.ppermute(from_left[:half], axis, ring_route(axis, 1))
    far_bottom = lax.ppermute(from_right[half:], axis, ring_route(axis, -1))
    far = jnp.concatenate([far_top, far_bottom], 0)
    pieces = [
        (local, index),
        (from_left, ring_place((place - 1) % count)),
        (from_right, ring_place((place + 1) % count)),
        (far, ring_place((place + 2) % count)),
    ]
    totals = [None] * len(weights)
    squares = None
    for piece, source in pieces:
        piece_f = piece.astype(jnp.float32)
        part_sq = jnp.sum(piece_f * piece_f, -1)
        squares = part_sq if squares is None else squares + part_sq
        for k, weight in enumerate(weights):
            rows = lax.dynamic_slice_in_dim(weight, source * width, width, 0)
            term = jnp.dot(piece, rows, preferred_element_type=jnp.float32)
            totals[k] = term if totals[k] is None else totals[k] + term
    return totals, squares


def direct_products(local, weights, axis):
    count, index = (lax.axis_size(axis), lax.axis_index(axis))
    width = local.shape[1]
    pieces = [(local, index)]
    for distance in range(1, count):
        route = [(i, (i + distance) % count) for i in range(count)]
        pieces.append((lax.ppermute(local, axis, route), (index - distance) % count))
    totals = [None] * len(weights)
    squares = None
    for piece, source in pieces:
        piece_f = piece.astype(jnp.float32)
        part_sq = jnp.sum(piece_f * piece_f, -1)
        squares = part_sq if squares is None else squares + part_sq
        for k, weight in enumerate(weights):
            rows = lax.dynamic_slice_in_dim(weight, source * width, width, 0)
            term = jnp.dot(piece, rows, preferred_element_type=jnp.float32)
            totals[k] = term if totals[k] is None else totals[k] + term
    return totals, squares


def scattered_sum(left, weight, axis):
    count, index = (lax.axis_size(axis), lax.axis_index(axis))
    width = weight.shape[1] // count
    place = ring_place(index)
    half = left.shape[0] // 2

    def block(owner_place, rows=slice(None)):
        owner = ring_place(owner_place % count)
        cols = lax.dynamic_slice_in_dim(weight, owner * width, width, 1)
        return jnp.dot(left[rows], cols, preferred_element_type=jnp.float32)

    relay_top = lax.ppermute(
        block(place + 2, slice(0, half)).astype(jnp.bfloat16), axis, ring_route(axis, 1)
    )
    relay_bottom = lax.ppermute(
        block(place + 2, slice(half, None)).astype(jnp.bfloat16), axis, ring_route(axis, -1)
    )
    right_block = block(place + 1).astype(jnp.bfloat16).astype(jnp.float32)
    right_block = jnp.concatenate(
        [right_block[:half] + relay_top.astype(jnp.float32), right_block[half:]], 0
    )
    left_block = block(place - 1).astype(jnp.bfloat16).astype(jnp.float32)
    left_block = jnp.concatenate(
        [left_block[:half], left_block[half:] + relay_bottom.astype(jnp.float32)], 0
    )
    from_left = lax.ppermute(right_block.astype(jnp.bfloat16), axis, ring_route(axis, 1))
    from_right = lax.ppermute(left_block.astype(jnp.bfloat16), axis, ring_route(axis, -1))
    own = block(place).astype(jnp.bfloat16).astype(jnp.float32)
    return own + from_left.astype(jnp.float32) + from_right.astype(jnp.float32)


def unit_rows(values_in):
    return values_in * lax.rsqrt(jnp.sum(values_in * values_in, -1, keepdims=True) + epsilon)


def exact_product(left, right):
    return jnp.matmul(left, right, precision=lax.Precision.HIGHEST)


def body(
    activations,
    seg_len,
    seg_start,
    memory_rates,
    w_qkv,
    conv_w,
    persistent,
    w_out,
    w_gate,
    w_up,
    w_down,
):
    token_rows, local_feat = activations.shape
    seg_count = seg_len.shape[0]
    full_width = w_qkv.shape[0]
    head_width = w_qkv.shape[2]
    local_heads = head_width // HD
    group_index = lax.axis_index(("tr", "tc"))
    wide = w_qkv.reshape(full_width, 3 * head_width)
    row_ids = jnp.arange(token_rows, dtype=jnp.int32)
    position = row_ids % SEG
    segment_of = row_ids // SEG
    continuing = seg_start[segment_of] == 0
    (projected,), squares = direct_products(activations, (wide,), ("tr", "tc"))
    qkv = (projected * lax.rsqrt(squares / full_width + epsilon)[:, None]).astype(jnp.bfloat16)
    edge_rows = passed_along(qkv[token_rows - (CONV - 1) :], "seq", 1)
    extended = jnp.concatenate([edge_rows, qkv], 0)
    taps = conv_w.reshape(CONV, 3 * head_width)
    convolved = jnp.zeros((token_rows, 3 * head_width), jnp.float32)
    for offset in range(CONV):
        shifted = extended[CONV - 1 - offset : CONV - 1 - offset + token_rows].astype(jnp.float32)
        valid = (position >= offset) | continuing
        convolved = convolved + jnp.where(valid[:, None], taps[offset] * shifted, 0.0)
    parts = convolved.reshape(token_rows, 3, local_heads, HD)
    query_n = unit_rows(parts[:, 0]).astype(jnp.bfloat16)
    key_n = unit_rows(parts[:, 1]).astype(jnp.bfloat16)
    value_n = parts[:, 2].astype(jnp.bfloat16)
    pkeys = unit_rows(persistent[0].astype(jnp.float32).reshape(-1, local_heads, HD)).astype(
        jnp.bfloat16
    )
    pvalues = persistent[1].reshape(-1, local_heads, HD)
    persist_rows = pkeys.shape[0]
    live = position < seg_len[segment_of]
    keys_live = jnp.where(live[:, None, None], key_n, jnp.zeros((), jnp.bfloat16)).reshape(
        seg_count, SEG, local_heads, HD
    )
    value_segs = value_n.reshape(seg_count, SEG, local_heads, HD)
    a_mats = jnp.einsum("cthi,cthj->chij", keys_live, keys_live, preferred_element_type=jnp.float32)
    b_mats = jnp.einsum(
        "cthi,cthj->chij", keys_live, value_segs, preferred_element_type=jnp.float32
    )
    my_rates = lax.dynamic_slice_in_dim(memory_rates, group_index * local_heads, local_heads, 2)
    decay_factor = my_rates[0][:, :, None, None]
    eta = my_rates[1][:, :, None, None]
    theta = my_rates[2][:, :, None, None]
    keep = (1 - seg_start).astype(jnp.float32)[:, None, None, None]
    identity = jnp.eye(HD, dtype=jnp.float32)
    upper = jnp.concatenate([(1.0 - decay_factor) * identity - theta * a_mats, eta * identity], -1)
    lower = jnp.concatenate([-theta * a_mats, eta * identity], -1)
    seg_maps = jnp.concatenate([upper, lower], -2) * keep
    seg_shifts = jnp.concatenate([theta * b_mats, theta * b_mats], -2)
    reach = min(PROMPT_SPAN, lax.axis_size("seq"))
    memory_in = memory_entering(seg_maps[0], seg_shifts[0], "seq", reach) * keep[0]
    query_seg = query_n.astype(jnp.float32)
    retr_parts = jnp.einsum("thi,hij->thj", query_seg, memory_in, precision=lax.Precision.HIGHEST)
    mem = retr_parts * lax.rsqrt(jnp.mean(retr_parts * retr_parts, -1, keepdims=True) + epsilon)
    block_rows = min(512, SEG)
    attn_parts = []
    seg_index = 0
    first = seg_index * SEG
    keys_all = jnp.concatenate([pkeys, key_n], 0)
    values_all = jnp.concatenate([pvalues, value_n], 0)
    cols_k = jnp.arange(persist_rows + SEG, dtype=jnp.int32)[None, :] - persist_rows
    for block_start in range(0, SEG, block_rows):
        query_blk = query_n[first + block_start : first + block_start + block_rows]
        scores = score_scale * jnp.einsum(
            "qhd,khd->hqk", query_blk, keys_all, preferred_element_type=jnp.float32
        )
        rows_q = block_start + jnp.arange(block_rows, dtype=jnp.int32)[:, None]
        allow = (cols_k < 0) | (cols_k <= rows_q) & (cols_k < seg_len[seg_index])
        weights = jnp.where(allow[None], jnp.exp(scores), 0.0)
        probs = (weights / jnp.sum(weights, -1, keepdims=True)).astype(jnp.bfloat16)
        attn_parts.append(
            jnp.einsum("hqk,khd->qhd", probs, values_all, preferred_element_type=jnp.float32)
        )
    attn = jnp.concatenate(attn_parts, 0)
    heads_out = (attn + mem).astype(jnp.bfloat16).reshape(token_rows, head_width)
    chunk = token_rows // FINISH_CHUNKS
    outs = []
    for first_row in range(0, token_rows, chunk):
        rows = slice(first_row, first_row + chunk)
        share = scattered_sum(heads_out[rows], w_out, ("tr", "tc"))
        resid = (activations[rows].astype(jnp.float32) + share).astype(jnp.bfloat16)
        (gate, up_proj), squares2 = gathered_products(resid, (w_gate, w_up), ("tr", "tc"))
        inv_rms2 = lax.rsqrt(squares2 / full_width + epsilon)[:, None]
        hidden = (jax.nn.silu(gate * inv_rms2) * (up_proj * inv_rms2)).astype(jnp.bfloat16)
        ffn_share = scattered_sum(hidden, w_down, ("tr", "tc"))
        outs.append((resid.astype(jnp.float32) + ffn_share).astype(jnp.bfloat16))
    return jnp.concatenate(outs, 0)


def solution(mesh):
    return jax.shard_map(
        body,
        mesh=mesh,
        in_specs=(
            P("seq", ("tr", "tc")),
            P("seq"),
            P("seq"),
            P(None, "seq", None),
            P(None, None, ("tr", "tc")),
            P(None, None, ("tr", "tc")),
            P(None, None, ("tr", "tc")),
            P(("tr", "tc"), None),
            P(None, ("tr", "tc")),
            P(None, ("tr", "tc")),
            P(("tr", "tc"), None),
        ),
        out_specs=P("seq", ("tr", "tc")),
        check_vma=False,
    )
```

```python
import jax
import jax.numpy as jnp
from jax import lax
from jax.sharding import PartitionSpec as P

HD = 128
SEG = 1024
CONV = 4
PROMPT_SPAN = 32
FINISH_CHUNKS = 2


epsilon = 1e-06
score_scale = 8.0


def passed_along(block, axis, distance):
    devices = range(lax.axis_size(axis))
    route = [(i - distance, i) for i in devices if i - distance in devices]
    return lax.ppermute(block, axis, route)


def exact_pair(block):
    high = block.astype(jnp.bfloat16)
    low = (block - high.astype(jnp.float32)).astype(jnp.bfloat16)
    return jnp.concatenate([high, low], -1)


def from_pair(pair):
    half = pair.shape[-1] // 2
    return pair[..., :half].astype(jnp.float32) + pair[..., half:].astype(jnp.float32)


def routed(block, axis, pairs):
    return lax.ppermute(block, axis, [(i, j) for i, j in pairs if 0 <= i])


def memory_entering(seg_map, seg_shift, axis, reach):
    count = lax.axis_size(axis)
    odd = lax.axis_index(axis) % 2 == 1
    width = seg_map.shape[-1]
    rows = seg_shift.shape[-1]
    payload = jnp.concatenate([seg_map, seg_shift], -1).astype(jnp.bfloat16)
    sibling = routed(payload, axis, [(i - 1, i) for i in range(1, count, 2)]).astype(jnp.float32)
    moved = exact_product(seg_map, sibling)
    pair_map = jnp.where(odd, moved[..., :width], seg_map)
    pair_shift = jnp.where(odd, moved[..., width:] + seg_shift, seg_shift)
    chips = 1
    while 4 * chips < reach:
        payload = jnp.concatenate([pair_map, pair_shift], -1).astype(jnp.bfloat16)
        arrived = routed(payload, axis, [(i - 2 * chips, i) for i in range(1, count, 2)])
        moved = exact_product(pair_map, arrived.astype(jnp.float32))
        pair_shift = moved[..., width:] + pair_shift
        pair_map = moved[..., :width]
        chips *= 2
    span = 2 * chips
    far = routed(pair_shift.astype(jnp.bfloat16), axis, [(i - span, i) for i in range(1, count, 2)])
    window = exact_product(pair_map, far.astype(jnp.float32)) + pair_shift
    to_even = from_pair(
        routed(exact_pair(window[:, :rows]), axis, [(i - 1, i) for i in range(2, count, 2)])
    )
    to_odd = from_pair(routed(exact_pair(window), axis, [(i - 2, i) for i in range(3, count, 2)]))
    sibling_map = sibling[..., :width][:, :rows]
    sibling_shift = sibling[..., width:][:, :rows]
    odd_state = exact_product(sibling_map, to_odd) + sibling_shift
    return jnp.where(odd, odd_state, to_even)


def ring_place(index):
    return (index % 2) * 2 + index // 2


def ring_route(axis, step):
    count = lax.axis_size(axis)
    return [(i, ring_place((ring_place(i) + step) % count)) for i in range(count)]


def gathered_products(local, weights, axis):
    count, index = (lax.axis_size(axis), lax.axis_index(axis))
    width = local.shape[1]
    place = ring_place(index)
    half = local.shape[0] // 2
    from_left = lax.ppermute(local, axis, ring_route(axis, 1))
    from_right = lax.ppermute(local, axis, ring_route(axis, -1))
    far_top = lax.ppermute(from_left[:half], axis, ring_route(axis, 1))
    far_bottom = lax.ppermute(from_right[half:], axis, ring_route(axis, -1))
    far = jnp.concatenate([far_top, far_bottom], 0)
    pieces = [
        (local, index),
        (from_left, ring_place((place - 1) % count)),
        (from_right, ring_place((place + 1) % count)),
        (far, ring_place((place + 2) % count)),
    ]
    totals = [None] * len(weights)
    squares = None
    for piece, source in pieces:
        piece_f = piece.astype(jnp.float32)
        part_sq = jnp.sum(piece_f * piece_f, -1)
        squares = part_sq if squares is None else squares + part_sq
        for k, weight in enumerate(weights):
            rows = lax.dynamic_slice_in_dim(weight, source * width, width, 0)
            term = jnp.dot(piece, rows, preferred_element_type=jnp.float32)
            totals[k] = term if totals[k] is None else totals[k] + term
    return totals, squares


def direct_products(local, weights, axis):
    count, index = (lax.axis_size(axis), lax.axis_index(axis))
    width = local.shape[1]
    pieces = [(local, index)]
    for distance in range(1, count):
        route = [(i, (i + distance) % count) for i in range(count)]
        pieces.append((lax.ppermute(local, axis, route), (index - distance) % count))
    totals = [None] * len(weights)
    squares = None
    for piece, source in pieces:
        piece_f = piece.astype(jnp.float32)
        part_sq = jnp.sum(piece_f * piece_f, -1)
        squares = part_sq if squares is None else squares + part_sq
        for k, weight in enumerate(weights):
            rows = lax.dynamic_slice_in_dim(weight, source * width, width, 0)
            term = jnp.dot(piece, rows, preferred_element_type=jnp.float32)
            totals[k] = term if totals[k] is None else totals[k] + term
    return totals, squares


def scattered_sum(left, weight, axis):
    count, index = (lax.axis_size(axis), lax.axis_index(axis))
    width = weight.shape[1] // count
    place = ring_place(index)
    half = left.shape[0] // 2

    def block(owner_place, rows=slice(None)):
        owner = ring_place(owner_place % count)
        cols = lax.dynamic_slice_in_dim(weight, owner * width, width, 1)
        return jnp.dot(left[rows], cols, preferred_element_type=jnp.float32)

    relay_top = lax.ppermute(
        block(place + 2, slice(0, half)).astype(jnp.bfloat16), axis, ring_route(axis, 1)
    )
    relay_bottom = lax.ppermute(
        block(place + 2, slice(half, None)).astype(jnp.bfloat16), axis, ring_route(axis, -1)
    )
    right_block = block(place + 1).astype(jnp.bfloat16).astype(jnp.float32)
    right_block = jnp.concatenate(
        [right_block[:half] + relay_top.astype(jnp.float32), right_block[half:]], 0
    )
    left_block = block(place - 1).astype(jnp.bfloat16).astype(jnp.float32)
    left_block = jnp.concatenate(
        [left_block[:half], left_block[half:] + relay_bottom.astype(jnp.float32)], 0
    )
    from_left = lax.ppermute(right_block.astype(jnp.bfloat16), axis, ring_route(axis, 1))
    from_right = lax.ppermute(left_block.astype(jnp.bfloat16), axis, ring_route(axis, -1))
    own = block(place).astype(jnp.bfloat16).astype(jnp.float32)
    return own + from_left.astype(jnp.float32) + from_right.astype(jnp.float32)


def unit_rows(values_in):
    return values_in * lax.rsqrt(jnp.sum(values_in * values_in, -1, keepdims=True) + epsilon)


def exact_product(left, right):
    return jnp.matmul(left, right, precision=lax.Precision.HIGHEST)


def body(
    activations,
    seg_len,
    seg_start,
    memory_rates,
    w_qkv,
    conv_w,
    persistent,
    w_out,
    w_gate,
    w_up,
    w_down,
):
    token_rows, local_feat = activations.shape
    seg_count = seg_len.shape[0]
    full_width = w_qkv.shape[0]
    head_width = w_qkv.shape[2]
    local_heads = head_width // HD
    group_index = lax.axis_index(("tr", "tc"))
    wide = w_qkv.reshape(full_width, 3 * head_width)
    row_ids = jnp.arange(token_rows, dtype=jnp.int32)
    position = row_ids % SEG
    segment_of = row_ids // SEG
    continuing = seg_start[segment_of] == 0
    (projected,), squares = direct_products(activations, (wide,), ("tr", "tc"))
    qkv = (projected * lax.rsqrt(squares / full_width + epsilon)[:, None]).astype(jnp.bfloat16)
    edge_rows = passed_along(qkv[token_rows - (CONV - 1) :], "seq", 1)
    extended = jnp.concatenate([edge_rows, qkv], 0)
    taps = conv_w.reshape(CONV, 3 * head_width)
    convolved = jnp.zeros((token_rows, 3 * head_width), jnp.float32)
    for offset in range(CONV):
        shifted = extended[CONV - 1 - offset : CONV - 1 - offset + token_rows].astype(jnp.float32)
        valid = (position >= offset) | continuing
        convolved = convolved + jnp.where(valid[:, None], taps[offset] * shifted, 0.0)
    parts = convolved.reshape(token_rows, 3, local_heads, HD)
    query_n = unit_rows(parts[:, 0]).astype(jnp.bfloat16)
    key_n = unit_rows(parts[:, 1]).astype(jnp.bfloat16)
    value_n = parts[:, 2].astype(jnp.bfloat16)
    pkeys = unit_rows(persistent[0].astype(jnp.float32).reshape(-1, local_heads, HD)).astype(
        jnp.bfloat16
    )
    pvalues = persistent[1].reshape(-1, local_heads, HD)
    persist_rows = pkeys.shape[0]
    live = position < seg_len[segment_of]
    keys_live = jnp.where(live[:, None, None], key_n, jnp.zeros((), jnp.bfloat16)).reshape(
        seg_count, SEG, local_heads, HD
    )
    value_segs = value_n.reshape(seg_count, SEG, local_heads, HD)
    a_mats = jnp.einsum("cthi,cthj->chij", keys_live, keys_live, preferred_element_type=jnp.float32)
    b_mats = jnp.einsum(
        "cthi,cthj->chij", keys_live, value_segs, preferred_element_type=jnp.float32
    )
    my_rates = lax.dynamic_slice_in_dim(memory_rates, group_index * local_heads, local_heads, 2)
    decay_factor = my_rates[0][:, :, None, None]
    eta = my_rates[1][:, :, None, None]
    theta = my_rates[2][:, :, None, None]
    keep = (1 - seg_start).astype(jnp.float32)[:, None, None, None]
    identity = jnp.eye(HD, dtype=jnp.float32)
    upper = jnp.concatenate([(1.0 - decay_factor) * identity - theta * a_mats, eta * identity], -1)
    lower = jnp.concatenate([-theta * a_mats, eta * identity], -1)
    seg_maps = jnp.concatenate([upper, lower], -2) * keep
    seg_shifts = jnp.concatenate([theta * b_mats, theta * b_mats], -2)
    reach = min(PROMPT_SPAN, lax.axis_size("seq"))
    memory_in = memory_entering(seg_maps[0], seg_shifts[0], "seq", reach) * keep[0]
    query_seg = query_n.astype(jnp.float32)
    retr_parts = jnp.einsum("thi,hij->thj", query_seg, memory_in, precision=lax.Precision.HIGHEST)
    mem = retr_parts * lax.rsqrt(jnp.mean(retr_parts * retr_parts, -1, keepdims=True) + epsilon)
    block_rows = min(512, SEG)
    attn_parts = []
    seg_index = 0
    first = seg_index * SEG
    keys_all = jnp.concatenate([pkeys, key_n], 0)
    values_all = jnp.concatenate([pvalues, value_n], 0)
    cols_k = jnp.arange(persist_rows + SEG, dtype=jnp.int32)[None, :] - persist_rows
    for block_start in range(0, SEG, block_rows):
        query_blk = query_n[first + block_start : first + block_start + block_rows]
        scores = score_scale * jnp.einsum(
            "qhd,khd->hqk", query_blk, keys_all, preferred_element_type=jnp.float32
        )
        rows_q = block_start + jnp.arange(block_rows, dtype=jnp.int32)[:, None]
        allow = (cols_k < 0) | (cols_k <= rows_q) & (cols_k < seg_len[seg_index])
        weights = jnp.where(allow[None], jnp.exp(scores), 0.0)
        probs = (weights / jnp.sum(weights, -1, keepdims=True)).astype(jnp.bfloat16)
        attn_parts.append(
            jnp.einsum("hqk,khd->qhd", probs, values_all, preferred_element_type=jnp.float32)
        )
    attn = jnp.concatenate(attn_parts, 0)
    heads_out = (attn + mem).astype(jnp.bfloat16).reshape(token_rows, head_width)
    chunk = token_rows // FINISH_CHUNKS
    outs = []
    for first_row in range(0, token_rows, chunk):
        rows = slice(first_row, first_row + chunk)
        share = scattered_sum(heads_out[rows], w_out, ("tr", "tc"))
        resid = (activations[rows].astype(jnp.float32) + share).astype(jnp.bfloat16)
        (gate, up_proj), squares2 = gathered_products(resid, (w_gate, w_up), ("tr", "tc"))
        inv_rms2 = lax.rsqrt(squares2 / full_width + epsilon)[:, None]
        hidden = (jax.nn.silu(gate * inv_rms2) * (up_proj * inv_rms2)).astype(jnp.bfloat16)
        ffn_share = scattered_sum(hidden, w_down, ("tr", "tc"))
        outs.append((resid.astype(jnp.float32) + ffn_share).astype(jnp.bfloat16))
    return jnp.concatenate(outs, 0)


def solution(mesh):
    return jax.shard_map(
        body,
        mesh=mesh,
        in_specs=(
            P("seq", ("tr", "tc")),
            P("seq"),
            P("seq"),
            P(None, "seq", None),
            P(None, None, ("tr", "tc")),
            P(None, None, ("tr", "tc")),
            P(None, None, ("tr", "tc")),
            P(("tr", "tc"), None),
            P(None, ("tr", "tc")),
            P(None, ("tr", "tc")),
            P(("tr", "tc"), None),
        ),
        out_specs=P("seq", ("tr", "tc")),
        check_vma=False,
    )
```

```python
import jax
import jax.numpy as jnp
from jax import lax
from jax.sharding import PartitionSpec as P

HD = 128
SEG = 1024
CONV = 4
PROMPT_SPAN = 32
FINISH_CHUNKS = 2


epsilon = 1e-06
score_scale = 8.0


def passed_along(block, axis, distance):
    devices = range(lax.axis_size(axis))
    route = [(i - distance, i) for i in devices if i - distance in devices]
    return lax.ppermute(block, axis, route)


def exact_pair(block):
    high = block.astype(jnp.bfloat16)
    low = (block - high.astype(jnp.float32)).astype(jnp.bfloat16)
    return jnp.concatenate([high, low], -1)


def from_pair(pair):
    half = pair.shape[-1] // 2
    return pair[..., :half].astype(jnp.float32) + pair[..., half:].astype(jnp.float32)


def routed(block, axis, pairs):
    return lax.ppermute(block, axis, [(i, j) for i, j in pairs if 0 <= i])


def memory_entering(seg_map, seg_shift, axis, reach):
    count = lax.axis_size(axis)
    odd = lax.axis_index(axis) % 2 == 1
    width = seg_map.shape[-1]
    rows = seg_shift.shape[-1]
    payload = jnp.concatenate([seg_map, seg_shift], -1).astype(jnp.bfloat16)
    sibling = routed(payload, axis, [(i - 1, i) for i in range(1, count, 2)]).astype(jnp.float32)
    moved = exact_product(seg_map, sibling)
    pair_map = jnp.where(odd, moved[..., :width], seg_map)
    pair_shift = jnp.where(odd, moved[..., width:] + seg_shift, seg_shift)
    chips = 1
    while 4 * chips < reach:
        payload = jnp.concatenate([pair_map, pair_shift], -1).astype(jnp.bfloat16)
        arrived = routed(payload, axis, [(i - 2 * chips, i) for i in range(1, count, 2)])
        moved = exact_product(pair_map, arrived.astype(jnp.float32))
        pair_shift = moved[..., width:] + pair_shift
        pair_map = moved[..., :width]
        chips *= 2
    span = 2 * chips
    far = routed(pair_shift.astype(jnp.bfloat16), axis, [(i - span, i) for i in range(1, count, 2)])
    window = exact_product(pair_map, far.astype(jnp.float32)) + pair_shift
    to_even = from_pair(
        routed(exact_pair(window[:, :rows]), axis, [(i - 1, i) for i in range(2, count, 2)])
    )
    to_odd = from_pair(routed(exact_pair(window), axis, [(i - 2, i) for i in range(3, count, 2)]))
    sibling_map = sibling[..., :width][:, :rows]
    sibling_shift = sibling[..., width:][:, :rows]
    odd_state = exact_product(sibling_map, to_odd) + sibling_shift
    return jnp.where(odd, odd_state, to_even)


def ring_place(index):
    return (index % 2) * 2 + index // 2


def ring_route(axis, step):
    count = lax.axis_size(axis)
    return [(i, ring_place((ring_place(i) + step) % count)) for i in range(count)]


def gathered_products(local, weights, axis):
    count, index = (lax.axis_size(axis), lax.axis_index(axis))
    width = local.shape[1]
    place = ring_place(index)
    half = local.shape[0] // 2
    from_left = lax.ppermute(local, axis, ring_route(axis, 1))
    from_right = lax.ppermute(local, axis, ring_route(axis, -1))
    far_top = lax.ppermute(from_left[:half], axis, ring_route(axis, 1))
    far_bottom = lax.ppermute(from_right[half:], axis, ring_route(axis, -1))
    far = jnp.concatenate([far_top, far_bottom], 0)
    pieces = [
        (local, index),
        (from_left, ring_place((place - 1) % count)),
        (from_right, ring_place((place + 1) % count)),
        (far, ring_place((place + 2) % count)),
    ]
    totals = [None] * len(weights)
    squares = None
    for piece, source in pieces:
        piece_f = piece.astype(jnp.float32)
        part_sq = jnp.sum(piece_f * piece_f, -1)
        squares = part_sq if squares is None else squares + part_sq
        for k, weight in enumerate(weights):
            rows = lax.dynamic_slice_in_dim(weight, source * width, width, 0)
            term = jnp.dot(piece, rows, preferred_element_type=jnp.float32)
            totals[k] = term if totals[k] is None else totals[k] + term
    return totals, squares


def direct_products(local, weights, axis):
    count, index = (lax.axis_size(axis), lax.axis_index(axis))
    width = local.shape[1]
    pieces = [(local, index)]
    for distance in range(1, count):
        route = [(i, (i + distance) % count) for i in range(count)]
        pieces.append((lax.ppermute(local, axis, route), (index - distance) % count))
    totals = [None] * len(weights)
    squares = None
    for piece, source in pieces:
        piece_f = piece.astype(jnp.float32)
        part_sq = jnp.sum(piece_f * piece_f, -1)
        squares = part_sq if squares is None else squares + part_sq
        for k, weight in enumerate(weights):
            rows = lax.dynamic_slice_in_dim(weight, source * width, width, 0)
            term = jnp.dot(piece, rows, preferred_element_type=jnp.float32)
            totals[k] = term if totals[k] is None else totals[k] + term
    return totals, squares


def direct_sum(left, weight, axis):
    count, index = (lax.axis_size(axis), lax.axis_index(axis))
    width = weight.shape[1] // count

    def block(owner):
        cols = lax.dynamic_slice_in_dim(weight, owner * width, width, 1)
        return jnp.dot(left, cols, preferred_element_type=jnp.float32).astype(jnp.bfloat16)

    total = block(index).astype(jnp.float32)
    for distance in range(1, count):
        route = [(i, (i + distance) % count) for i in range(count)]
        arrived = lax.ppermute(block((index + distance) % count), axis, route)
        total = total + arrived.astype(jnp.float32)
    return total


def scattered_sum(left, weight, axis):
    count, index = (lax.axis_size(axis), lax.axis_index(axis))
    width = weight.shape[1] // count
    place = ring_place(index)
    half = left.shape[0] // 2

    def block(owner_place, rows=slice(None)):
        owner = ring_place(owner_place % count)
        cols = lax.dynamic_slice_in_dim(weight, owner * width, width, 1)
        return jnp.dot(left[rows], cols, preferred_element_type=jnp.float32)

    relay_top = lax.ppermute(
        block(place + 2, slice(0, half)).astype(jnp.bfloat16), axis, ring_route(axis, 1)
    )
    relay_bottom = lax.ppermute(
        block(place + 2, slice(half, None)).astype(jnp.bfloat16), axis, ring_route(axis, -1)
    )
    right_block = block(place + 1).astype(jnp.bfloat16).astype(jnp.float32)
    right_block = jnp.concatenate(
        [right_block[:half] + relay_top.astype(jnp.float32), right_block[half:]], 0
    )
    left_block = block(place - 1).astype(jnp.bfloat16).astype(jnp.float32)
    left_block = jnp.concatenate(
        [left_block[:half], left_block[half:] + relay_bottom.astype(jnp.float32)], 0
    )
    from_left = lax.ppermute(right_block.astype(jnp.bfloat16), axis, ring_route(axis, 1))
    from_right = lax.ppermute(left_block.astype(jnp.bfloat16), axis, ring_route(axis, -1))
    own = block(place).astype(jnp.bfloat16).astype(jnp.float32)
    return own + from_left.astype(jnp.float32) + from_right.astype(jnp.float32)


def unit_rows(values_in):
    return values_in * lax.rsqrt(jnp.sum(values_in * values_in, -1, keepdims=True) + epsilon)


def exact_product(left, right):
    return jnp.matmul(left, right, precision=lax.Precision.HIGHEST)


def body(
    activations,
    seg_len,
    seg_start,
    memory_rates,
    w_qkv,
    conv_w,
    persistent,
    w_out,
    w_gate,
    w_up,
    w_down,
):
    token_rows, local_feat = activations.shape
    seg_count = seg_len.shape[0]
    full_width = w_qkv.shape[0]
    head_width = w_qkv.shape[2]
    local_heads = head_width // HD
    group_index = lax.axis_index(("tr", "tc"))
    wide = w_qkv.reshape(full_width, 3 * head_width)
    row_ids = jnp.arange(token_rows, dtype=jnp.int32)
    position = row_ids % SEG
    segment_of = row_ids // SEG
    continuing = seg_start[segment_of] == 0
    (projected,), squares = direct_products(activations, (wide,), ("tr", "tc"))
    qkv = (projected * lax.rsqrt(squares / full_width + epsilon)[:, None]).astype(jnp.bfloat16)
    edge_rows = passed_along(qkv[token_rows - (CONV - 1) :], "seq", 1)
    extended = jnp.concatenate([edge_rows, qkv], 0)
    taps = conv_w.reshape(CONV, 3 * head_width)
    convolved = jnp.zeros((token_rows, 3 * head_width), jnp.float32)
    for offset in range(CONV):
        shifted = extended[CONV - 1 - offset : CONV - 1 - offset + token_rows].astype(jnp.float32)
        valid = (position >= offset) | continuing
        convolved = convolved + jnp.where(valid[:, None], taps[offset] * shifted, 0.0)
    parts = convolved.reshape(token_rows, 3, local_heads, HD)
    query_n = unit_rows(parts[:, 0]).astype(jnp.bfloat16)
    key_n = unit_rows(parts[:, 1]).astype(jnp.bfloat16)
    value_n = parts[:, 2].astype(jnp.bfloat16)
    pkeys = unit_rows(persistent[0].astype(jnp.float32).reshape(-1, local_heads, HD)).astype(
        jnp.bfloat16
    )
    pvalues = persistent[1].reshape(-1, local_heads, HD)
    persist_rows = pkeys.shape[0]
    live = position < seg_len[segment_of]
    keys_live = jnp.where(live[:, None, None], key_n, jnp.zeros((), jnp.bfloat16)).reshape(
        seg_count, SEG, local_heads, HD
    )
    value_segs = value_n.reshape(seg_count, SEG, local_heads, HD)
    a_mats = jnp.einsum("cthi,cthj->chij", keys_live, keys_live, preferred_element_type=jnp.float32)
    b_mats = jnp.einsum(
        "cthi,cthj->chij", keys_live, value_segs, preferred_element_type=jnp.float32
    )
    my_rates = lax.dynamic_slice_in_dim(memory_rates, group_index * local_heads, local_heads, 2)
    decay_factor = my_rates[0][:, :, None, None]
    eta = my_rates[1][:, :, None, None]
    theta = my_rates[2][:, :, None, None]
    keep = (1 - seg_start).astype(jnp.float32)[:, None, None, None]
    identity = jnp.eye(HD, dtype=jnp.float32)
    upper = jnp.concatenate([(1.0 - decay_factor) * identity - theta * a_mats, eta * identity], -1)
    lower = jnp.concatenate([-theta * a_mats, eta * identity], -1)
    seg_maps = jnp.concatenate([upper, lower], -2) * keep
    seg_shifts = jnp.concatenate([theta * b_mats, theta * b_mats], -2)
    reach = min(PROMPT_SPAN, lax.axis_size("seq"))
    memory_in = memory_entering(seg_maps[0], seg_shifts[0], "seq", reach) * keep[0]
    query_seg = query_n.astype(jnp.float32)
    retr_parts = jnp.einsum("thi,hij->thj", query_seg, memory_in, precision=lax.Precision.HIGHEST)
    mem = retr_parts * lax.rsqrt(jnp.mean(retr_parts * retr_parts, -1, keepdims=True) + epsilon)
    block_rows = min(512, SEG)
    attn_parts = []
    seg_index = 0
    first = seg_index * SEG
    keys_all = jnp.concatenate([pkeys, key_n], 0)
    values_all = jnp.concatenate([pvalues, value_n], 0)
    cols_k = jnp.arange(persist_rows + SEG, dtype=jnp.int32)[None, :] - persist_rows
    for block_start in range(0, SEG, block_rows):
        query_blk = query_n[first + block_start : first + block_start + block_rows]
        scores = score_scale * jnp.einsum(
            "qhd,khd->hqk", query_blk, keys_all, preferred_element_type=jnp.float32
        )
        rows_q = block_start + jnp.arange(block_rows, dtype=jnp.int32)[:, None]
        allow = (cols_k < 0) | (cols_k <= rows_q) & (cols_k < seg_len[seg_index])
        weights = jnp.where(allow[None], jnp.exp(scores), 0.0)
        probs = (weights / jnp.sum(weights, -1, keepdims=True)).astype(jnp.bfloat16)
        attn_parts.append(
            jnp.einsum("hqk,khd->qhd", probs, values_all, preferred_element_type=jnp.float32)
        )
    attn = jnp.concatenate(attn_parts, 0)
    heads_out = (attn + mem).astype(jnp.bfloat16).reshape(token_rows, head_width)
    chunk = token_rows // FINISH_CHUNKS
    outs = []
    for first_row in range(0, token_rows, chunk):
        rows = slice(first_row, first_row + chunk)
        share = direct_sum(heads_out[rows], w_out, ("tr", "tc"))
        resid = (activations[rows].astype(jnp.float32) + share).astype(jnp.bfloat16)
        (gate, up_proj), squares2 = direct_products(resid, (w_gate, w_up), ("tr", "tc"))
        inv_rms2 = lax.rsqrt(squares2 / full_width + epsilon)[:, None]
        hidden = (jax.nn.silu(gate * inv_rms2) * (up_proj * inv_rms2)).astype(jnp.bfloat16)
        ffn_share = direct_sum(hidden, w_down, ("tr", "tc"))
        outs.append((resid.astype(jnp.float32) + ffn_share).astype(jnp.bfloat16))
    return jnp.concatenate(outs, 0)


def solution(mesh):
    return jax.shard_map(
        body,
        mesh=mesh,
        in_specs=(
            P("seq", ("tr", "tc")),
            P("seq"),
            P("seq"),
            P(None, "seq", None),
            P(None, None, ("tr", "tc")),
            P(None, None, ("tr", "tc")),
            P(None, None, ("tr", "tc")),
            P(("tr", "tc"), None),
            P(None, ("tr", "tc")),
            P(None, ("tr", "tc")),
            P(("tr", "tc"), None),
        ),
        out_specs=P("seq", ("tr", "tc")),
        check_vma=False,
    )
```

```python
import jax
import jax.numpy as jnp
from jax import lax
from jax.sharding import PartitionSpec as P

HD = 128
SEG = 1024
CONV = 4
PROMPT_SPAN = 32
FINISH_CHUNKS = 2


epsilon = 1e-06
score_scale = 8.0


def passed_along(block, axis, distance):
    devices = range(lax.axis_size(axis))
    route = [(i - distance, i) for i in devices if i - distance in devices]
    return lax.ppermute(block, axis, route)


def exact_pair(block):
    high = block.astype(jnp.bfloat16)
    low = (block - high.astype(jnp.float32)).astype(jnp.bfloat16)
    return jnp.concatenate([high, low], -1)


def from_pair(pair):
    half = pair.shape[-1] // 2
    return pair[..., :half].astype(jnp.float32) + pair[..., half:].astype(jnp.float32)


def routed(block, axis, pairs):
    return lax.ppermute(block, axis, [(i, j) for i, j in pairs if 0 <= i])


def memory_entering(seg_map, seg_shift, axis, reach):
    count = lax.axis_size(axis)
    odd = lax.axis_index(axis) % 2 == 1
    width = seg_map.shape[-1]
    rows = seg_shift.shape[-1]
    payload = jnp.concatenate([seg_map, seg_shift], -1).astype(jnp.bfloat16)
    sibling = routed(payload, axis, [(i - 1, i) for i in range(1, count, 2)]).astype(jnp.float32)
    moved = exact_product(seg_map, sibling)
    pair_map = jnp.where(odd, moved[..., :width], seg_map)
    pair_shift = jnp.where(odd, moved[..., width:] + seg_shift, seg_shift)
    chips = 1
    while 4 * chips < reach:
        payload = jnp.concatenate([pair_map, pair_shift], -1).astype(jnp.bfloat16)
        arrived = routed(payload, axis, [(i - 2 * chips, i) for i in range(1, count, 2)])
        moved = exact_product(pair_map, arrived.astype(jnp.float32))
        pair_shift = moved[..., width:] + pair_shift
        pair_map = moved[..., :width]
        chips *= 2
    span = 2 * chips
    far = routed(pair_shift.astype(jnp.bfloat16), axis, [(i - span, i) for i in range(1, count, 2)])
    window = exact_product(pair_map, far.astype(jnp.float32)) + pair_shift
    to_even = from_pair(
        routed(exact_pair(window[:, :rows]), axis, [(i - 1, i) for i in range(2, count, 2)])
    )
    to_odd = from_pair(routed(exact_pair(window), axis, [(i - 2, i) for i in range(3, count, 2)]))
    sibling_map = sibling[..., :width][:, :rows]
    sibling_shift = sibling[..., width:][:, :rows]
    odd_state = exact_product(sibling_map, to_odd) + sibling_shift
    return jnp.where(odd, odd_state, to_even)


def ring_place(index):
    return (index % 2) * 2 + index // 2


def ring_route(axis, step):
    count = lax.axis_size(axis)
    return [(i, ring_place((ring_place(i) + step) % count)) for i in range(count)]


def gathered_products(local, weights, axis):
    count, index = (lax.axis_size(axis), lax.axis_index(axis))
    width = local.shape[1]
    place = ring_place(index)
    half = local.shape[0] // 2
    from_left = lax.ppermute(local, axis, ring_route(axis, 1))
    from_right = lax.ppermute(local, axis, ring_route(axis, -1))
    far_top = lax.ppermute(from_left[:half], axis, ring_route(axis, 1))
    far_bottom = lax.ppermute(from_right[half:], axis, ring_route(axis, -1))
    far = jnp.concatenate([far_top, far_bottom], 0)
    pieces = [
        (local, index),
        (from_left, ring_place((place - 1) % count)),
        (from_right, ring_place((place + 1) % count)),
        (far, ring_place((place + 2) % count)),
    ]
    totals = [None] * len(weights)
    squares = None
    for piece, source in pieces:
        piece_f = piece.astype(jnp.float32)
        part_sq = jnp.sum(piece_f * piece_f, -1)
        squares = part_sq if squares is None else squares + part_sq
        for k, weight in enumerate(weights):
            rows = lax.dynamic_slice_in_dim(weight, source * width, width, 0)
            term = jnp.dot(piece, rows, preferred_element_type=jnp.float32)
            totals[k] = term if totals[k] is None else totals[k] + term
    return totals, squares


def direct_products(local, weights, axis):
    count, index = (lax.axis_size(axis), lax.axis_index(axis))
    width = local.shape[1]
    pieces = [(local, index)]
    for distance in range(1, count):
        route = [(i, (i + distance) % count) for i in range(count)]
        pieces.append((lax.ppermute(local, axis, route), (index - distance) % count))
    totals = [None] * len(weights)
    squares = None
    for piece, source in pieces:
        piece_f = piece.astype(jnp.float32)
        part_sq = jnp.sum(piece_f * piece_f, -1)
        squares = part_sq if squares is None else squares + part_sq
        for k, weight in enumerate(weights):
            rows = lax.dynamic_slice_in_dim(weight, source * width, width, 0)
            term = jnp.dot(piece, rows, preferred_element_type=jnp.float32)
            totals[k] = term if totals[k] is None else totals[k] + term
    return totals, squares


def direct_sum(left, weight, axis):
    count, index = (lax.axis_size(axis), lax.axis_index(axis))
    width = weight.shape[1] // count

    def block(owner):
        cols = lax.dynamic_slice_in_dim(weight, owner * width, width, 1)
        return jnp.dot(left, cols, preferred_element_type=jnp.float32).astype(jnp.bfloat16)

    total = block(index).astype(jnp.float32)
    for distance in range(1, count):
        route = [(i, (i + distance) % count) for i in range(count)]
        arrived = lax.ppermute(block((index + distance) % count), axis, route)
        total = total + arrived.astype(jnp.float32)
    return total


def scattered_sum(left, weight, axis):
    count, index = (lax.axis_size(axis), lax.axis_index(axis))
    width = weight.shape[1] // count
    place = ring_place(index)
    half = left.shape[0] // 2

    def block(owner_place, rows=slice(None)):
        owner = ring_place(owner_place % count)
        cols = lax.dynamic_slice_in_dim(weight, owner * width, width, 1)
        return jnp.dot(left[rows], cols, preferred_element_type=jnp.float32)

    relay_top = lax.ppermute(
        block(place + 2, slice(0, half)).astype(jnp.bfloat16), axis, ring_route(axis, 1)
    )
    relay_bottom = lax.ppermute(
        block(place + 2, slice(half, None)).astype(jnp.bfloat16), axis, ring_route(axis, -1)
    )
    right_block = block(place + 1).astype(jnp.bfloat16).astype(jnp.float32)
    right_block = jnp.concatenate(
        [right_block[:half] + relay_top.astype(jnp.float32), right_block[half:]], 0
    )
    left_block = block(place - 1).astype(jnp.bfloat16).astype(jnp.float32)
    left_block = jnp.concatenate(
        [left_block[:half], left_block[half:] + relay_bottom.astype(jnp.float32)], 0
    )
    from_left = lax.ppermute(right_block.astype(jnp.bfloat16), axis, ring_route(axis, 1))
    from_right = lax.ppermute(left_block.astype(jnp.bfloat16), axis, ring_route(axis, -1))
    own = block(place).astype(jnp.bfloat16).astype(jnp.float32)
    return own + from_left.astype(jnp.float32) + from_right.astype(jnp.float32)


def unit_rows(values_in):
    return values_in * lax.rsqrt(jnp.sum(values_in * values_in, -1, keepdims=True) + epsilon)


def exact_product(left, right):
    return jnp.matmul(left, right, precision=lax.Precision.HIGHEST)


def body(
    activations,
    seg_len,
    seg_start,
    memory_rates,
    w_qkv,
    conv_w,
    persistent,
    w_out,
    w_gate,
    w_up,
    w_down,
):
    token_rows, local_feat = activations.shape
    seg_count = seg_len.shape[0]
    full_width = w_qkv.shape[0]
    head_width = w_qkv.shape[2]
    local_heads = head_width // HD
    group_index = lax.axis_index(("tr", "tc"))
    wide = w_qkv.reshape(full_width, 3 * head_width)
    row_ids = jnp.arange(token_rows, dtype=jnp.int32)
    position = row_ids % SEG
    segment_of = row_ids // SEG
    continuing = seg_start[segment_of] == 0
    (projected,), squares = direct_products(activations, (wide,), ("tr", "tc"))
    qkv = (projected * lax.rsqrt(squares / full_width + epsilon)[:, None]).astype(jnp.bfloat16)
    edge_rows = passed_along(qkv[token_rows - (CONV - 1) :], "seq", 1)
    extended = jnp.concatenate([edge_rows, qkv], 0)
    taps = conv_w.reshape(CONV, 3 * head_width)
    convolved = jnp.zeros((token_rows, 3 * head_width), jnp.float32)
    for offset in range(CONV):
        shifted = extended[CONV - 1 - offset : CONV - 1 - offset + token_rows].astype(jnp.float32)
        valid = (position >= offset) | continuing
        convolved = convolved + jnp.where(valid[:, None], taps[offset] * shifted, 0.0)
    parts = convolved.reshape(token_rows, 3, local_heads, HD)
    query_n = unit_rows(parts[:, 0]).astype(jnp.bfloat16)
    key_n = unit_rows(parts[:, 1]).astype(jnp.bfloat16)
    value_n = parts[:, 2].astype(jnp.bfloat16)
    pkeys = unit_rows(persistent[0].astype(jnp.float32).reshape(-1, local_heads, HD)).astype(
        jnp.bfloat16
    )
    pvalues = persistent[1].reshape(-1, local_heads, HD)
    persist_rows = pkeys.shape[0]
    live = position < seg_len[segment_of]
    keys_live = jnp.where(live[:, None, None], key_n, jnp.zeros((), jnp.bfloat16)).reshape(
        seg_count, SEG, local_heads, HD
    )
    value_segs = value_n.reshape(seg_count, SEG, local_heads, HD)
    a_mats = jnp.einsum("cthi,cthj->chij", keys_live, keys_live, preferred_element_type=jnp.float32)
    b_mats = jnp.einsum(
        "cthi,cthj->chij", keys_live, value_segs, preferred_element_type=jnp.float32
    )
    my_rates = lax.dynamic_slice_in_dim(memory_rates, group_index * local_heads, local_heads, 2)
    decay_factor = my_rates[0][:, :, None, None]
    eta = my_rates[1][:, :, None, None]
    theta = my_rates[2][:, :, None, None]
    keep = (1 - seg_start).astype(jnp.float32)[:, None, None, None]
    identity = jnp.eye(HD, dtype=jnp.float32)
    upper = jnp.concatenate([(1.0 - decay_factor) * identity - theta * a_mats, eta * identity], -1)
    lower = jnp.concatenate([-theta * a_mats, eta * identity], -1)
    seg_maps = jnp.concatenate([upper, lower], -2) * keep
    seg_shifts = jnp.concatenate([theta * b_mats, theta * b_mats], -2)
    reach = min(PROMPT_SPAN, lax.axis_size("seq"))
    memory_in = memory_entering(seg_maps[0], seg_shifts[0], "seq", reach) * keep[0]
    query_seg = query_n.astype(jnp.float32)
    retr_parts = jnp.einsum("thi,hij->thj", query_seg, memory_in, precision=lax.Precision.HIGHEST)
    mem = retr_parts * lax.rsqrt(jnp.mean(retr_parts * retr_parts, -1, keepdims=True) + epsilon)
    block_rows = SEG
    attn_parts = []
    seg_index = 0
    first = seg_index * SEG
    keys_all = jnp.concatenate([pkeys, key_n], 0)
    values_all = jnp.concatenate([pvalues, value_n], 0)
    cols_k = jnp.arange(persist_rows + SEG, dtype=jnp.int32)[None, :] - persist_rows
    for block_start in range(0, SEG, block_rows):
        query_blk = query_n[first + block_start : first + block_start + block_rows]
        scores = score_scale * jnp.einsum(
            "qhd,khd->hqk", query_blk, keys_all, preferred_element_type=jnp.float32
        )
        rows_q = block_start + jnp.arange(block_rows, dtype=jnp.int32)[:, None]
        allow = (cols_k < 0) | (cols_k <= rows_q) & (cols_k < seg_len[seg_index])
        weights = jnp.where(allow[None], jnp.exp(scores), 0.0)
        probs = (weights / jnp.sum(weights, -1, keepdims=True)).astype(jnp.bfloat16)
        attn_parts.append(
            jnp.einsum("hqk,khd->qhd", probs, values_all, preferred_element_type=jnp.float32)
        )
    attn = jnp.concatenate(attn_parts, 0)
    heads_out = (attn + mem).astype(jnp.bfloat16).reshape(token_rows, head_width)
    chunk = token_rows // FINISH_CHUNKS
    outs = []
    for first_row in range(0, token_rows, chunk):
        rows = slice(first_row, first_row + chunk)
        share = direct_sum(heads_out[rows], w_out, ("tr", "tc"))
        resid = (activations[rows].astype(jnp.float32) + share).astype(jnp.bfloat16)
        (gate, up_proj), squares2 = direct_products(resid, (w_gate, w_up), ("tr", "tc"))
        inv_rms2 = lax.rsqrt(squares2 / full_width + epsilon)[:, None]
        hidden = (jax.nn.silu(gate * inv_rms2) * (up_proj * inv_rms2)).astype(jnp.bfloat16)
        ffn_share = direct_sum(hidden, w_down, ("tr", "tc"))
        outs.append((resid.astype(jnp.float32) + ffn_share).astype(jnp.bfloat16))
    return jnp.concatenate(outs, 0)


def solution(mesh):
    return jax.shard_map(
        body,
        mesh=mesh,
        in_specs=(
            P("seq", ("tr", "tc")),
            P("seq"),
            P("seq"),
            P(None, "seq", None),
            P(None, None, ("tr", "tc")),
            P(None, None, ("tr", "tc")),
            P(None, None, ("tr", "tc")),
            P(("tr", "tc"), None),
            P(None, ("tr", "tc")),
            P(None, ("tr", "tc")),
            P(("tr", "tc"), None),
        ),
        out_specs=P("seq", ("tr", "tc")),
        check_vma=False,
    )
```

```python
import jax
import jax.numpy as jnp
from jax import lax
from jax.sharding import PartitionSpec as P

HD = 128
SEG = 1024
CONV = 4
PROMPT_SPAN = 32
FINISH_CHUNKS = 4


epsilon = 1e-06
score_scale = 8.0


def passed_along(block, axis, distance):
    devices = range(lax.axis_size(axis))
    route = [(i - distance, i) for i in devices if i - distance in devices]
    return lax.ppermute(block, axis, route)


def exact_pair(block):
    high = block.astype(jnp.bfloat16)
    low = (block - high.astype(jnp.float32)).astype(jnp.bfloat16)
    return jnp.concatenate([high, low], -1)


def from_pair(pair):
    half = pair.shape[-1] // 2
    return pair[..., :half].astype(jnp.float32) + pair[..., half:].astype(jnp.float32)


def routed(block, axis, pairs):
    return lax.ppermute(block, axis, [(i, j) for i, j in pairs if 0 <= i])


def memory_entering(seg_map, seg_shift, axis, reach):
    count = lax.axis_size(axis)
    odd = lax.axis_index(axis) % 2 == 1
    width = seg_map.shape[-1]
    rows = seg_shift.shape[-1]
    payload = jnp.concatenate([seg_map, seg_shift], -1).astype(jnp.bfloat16)
    sibling = routed(payload, axis, [(i - 1, i) for i in range(1, count, 2)]).astype(jnp.float32)
    moved = exact_product(seg_map, sibling)
    pair_map = jnp.where(odd, moved[..., :width], seg_map)
    pair_shift = jnp.where(odd, moved[..., width:] + seg_shift, seg_shift)
    chips = 1
    while 4 * chips < reach:
        payload = jnp.concatenate([pair_map, pair_shift], -1).astype(jnp.bfloat16)
        arrived = routed(payload, axis, [(i - 2 * chips, i) for i in range(1, count, 2)])
        moved = exact_product(pair_map, arrived.astype(jnp.float32))
        pair_shift = moved[..., width:] + pair_shift
        pair_map = moved[..., :width]
        chips *= 2
    span = 2 * chips
    far = routed(pair_shift.astype(jnp.bfloat16), axis, [(i - span, i) for i in range(1, count, 2)])
    window = exact_product(pair_map, far.astype(jnp.float32)) + pair_shift
    to_even = from_pair(
        routed(exact_pair(window[:, :rows]), axis, [(i - 1, i) for i in range(2, count, 2)])
    )
    to_odd = from_pair(routed(exact_pair(window), axis, [(i - 2, i) for i in range(3, count, 2)]))
    sibling_map = sibling[..., :width][:, :rows]
    sibling_shift = sibling[..., width:][:, :rows]
    odd_state = exact_product(sibling_map, to_odd) + sibling_shift
    return jnp.where(odd, odd_state, to_even)


def ring_place(index):
    return (index % 2) * 2 + index // 2


def ring_route(axis, step):
    count = lax.axis_size(axis)
    return [(i, ring_place((ring_place(i) + step) % count)) for i in range(count)]


def gathered_products(local, weights, axis):
    count, index = (lax.axis_size(axis), lax.axis_index(axis))
    width = local.shape[1]
    place = ring_place(index)
    half = local.shape[0] // 2
    from_left = lax.ppermute(local, axis, ring_route(axis, 1))
    from_right = lax.ppermute(local, axis, ring_route(axis, -1))
    far_top = lax.ppermute(from_left[:half], axis, ring_route(axis, 1))
    far_bottom = lax.ppermute(from_right[half:], axis, ring_route(axis, -1))
    far = jnp.concatenate([far_top, far_bottom], 0)
    pieces = [
        (local, index),
        (from_left, ring_place((place - 1) % count)),
        (from_right, ring_place((place + 1) % count)),
        (far, ring_place((place + 2) % count)),
    ]
    totals = [None] * len(weights)
    squares = None
    for piece, source in pieces:
        piece_f = piece.astype(jnp.float32)
        part_sq = jnp.sum(piece_f * piece_f, -1)
        squares = part_sq if squares is None else squares + part_sq
        for k, weight in enumerate(weights):
            rows = lax.dynamic_slice_in_dim(weight, source * width, width, 0)
            term = jnp.dot(piece, rows, preferred_element_type=jnp.float32)
            totals[k] = term if totals[k] is None else totals[k] + term
    return totals, squares


def direct_products(local, weights, axis):
    count, index = (lax.axis_size(axis), lax.axis_index(axis))
    width = local.shape[1]
    pieces = [(local, index)]
    for distance in range(1, count):
        route = [(i, (i + distance) % count) for i in range(count)]
        pieces.append((lax.ppermute(local, axis, route), (index - distance) % count))
    totals = [None] * len(weights)
    squares = None
    for piece, source in pieces:
        piece_f = piece.astype(jnp.float32)
        part_sq = jnp.sum(piece_f * piece_f, -1)
        squares = part_sq if squares is None else squares + part_sq
        for k, weight in enumerate(weights):
            rows = lax.dynamic_slice_in_dim(weight, source * width, width, 0)
            term = jnp.dot(piece, rows, preferred_element_type=jnp.float32)
            totals[k] = term if totals[k] is None else totals[k] + term
    return totals, squares


def direct_sum(left, weight, axis):
    count, index = (lax.axis_size(axis), lax.axis_index(axis))
    width = weight.shape[1] // count

    def block(owner):
        cols = lax.dynamic_slice_in_dim(weight, owner * width, width, 1)
        return jnp.dot(left, cols, preferred_element_type=jnp.float32).astype(jnp.bfloat16)

    total = block(index).astype(jnp.float32)
    for distance in range(1, count):
        route = [(i, (i + distance) % count) for i in range(count)]
        arrived = lax.ppermute(block((index + distance) % count), axis, route)
        total = total + arrived.astype(jnp.float32)
    return total


def scattered_sum(left, weight, axis):
    count, index = (lax.axis_size(axis), lax.axis_index(axis))
    width = weight.shape[1] // count
    place = ring_place(index)
    half = left.shape[0] // 2

    def block(owner_place, rows=slice(None)):
        owner = ring_place(owner_place % count)
        cols = lax.dynamic_slice_in_dim(weight, owner * width, width, 1)
        return jnp.dot(left[rows], cols, preferred_element_type=jnp.float32)

    relay_top = lax.ppermute(
        block(place + 2, slice(0, half)).astype(jnp.bfloat16), axis, ring_route(axis, 1)
    )
    relay_bottom = lax.ppermute(
        block(place + 2, slice(half, None)).astype(jnp.bfloat16), axis, ring_route(axis, -1)
    )
    right_block = block(place + 1).astype(jnp.bfloat16).astype(jnp.float32)
    right_block = jnp.concatenate(
        [right_block[:half] + relay_top.astype(jnp.float32), right_block[half:]], 0
    )
    left_block = block(place - 1).astype(jnp.bfloat16).astype(jnp.float32)
    left_block = jnp.concatenate(
        [left_block[:half], left_block[half:] + relay_bottom.astype(jnp.float32)], 0
    )
    from_left = lax.ppermute(right_block.astype(jnp.bfloat16), axis, ring_route(axis, 1))
    from_right = lax.ppermute(left_block.astype(jnp.bfloat16), axis, ring_route(axis, -1))
    own = block(place).astype(jnp.bfloat16).astype(jnp.float32)
    return own + from_left.astype(jnp.float32) + from_right.astype(jnp.float32)


def unit_rows(values_in):
    return values_in * lax.rsqrt(jnp.sum(values_in * values_in, -1, keepdims=True) + epsilon)


def exact_product(left, right):
    return jnp.matmul(left, right, precision=lax.Precision.HIGHEST)


def body(
    activations,
    seg_len,
    seg_start,
    memory_rates,
    w_qkv,
    conv_w,
    persistent,
    w_out,
    w_gate,
    w_up,
    w_down,
):
    token_rows, local_feat = activations.shape
    seg_count = seg_len.shape[0]
    full_width = w_qkv.shape[0]
    head_width = w_qkv.shape[2]
    local_heads = head_width // HD
    group_index = lax.axis_index(("tr", "tc"))
    wide = w_qkv.reshape(full_width, 3 * head_width)
    row_ids = jnp.arange(token_rows, dtype=jnp.int32)
    position = row_ids % SEG
    segment_of = row_ids // SEG
    continuing = seg_start[segment_of] == 0
    (projected,), squares = direct_products(activations, (wide,), ("tr", "tc"))
    qkv = (projected * lax.rsqrt(squares / full_width + epsilon)[:, None]).astype(jnp.bfloat16)
    edge_rows = passed_along(qkv[token_rows - (CONV - 1) :], "seq", 1)
    extended = jnp.concatenate([edge_rows, qkv], 0)
    taps = conv_w.reshape(CONV, 3 * head_width)
    convolved = jnp.zeros((token_rows, 3 * head_width), jnp.float32)
    for offset in range(CONV):
        shifted = extended[CONV - 1 - offset : CONV - 1 - offset + token_rows].astype(jnp.float32)
        valid = (position >= offset) | continuing
        convolved = convolved + jnp.where(valid[:, None], taps[offset] * shifted, 0.0)
    parts = convolved.reshape(token_rows, 3, local_heads, HD)
    query_n = unit_rows(parts[:, 0]).astype(jnp.bfloat16)
    key_n = unit_rows(parts[:, 1]).astype(jnp.bfloat16)
    value_n = parts[:, 2].astype(jnp.bfloat16)
    pkeys = unit_rows(persistent[0].astype(jnp.float32).reshape(-1, local_heads, HD)).astype(
        jnp.bfloat16
    )
    pvalues = persistent[1].reshape(-1, local_heads, HD)
    persist_rows = pkeys.shape[0]
    live = position < seg_len[segment_of]
    keys_live = jnp.where(live[:, None, None], key_n, jnp.zeros((), jnp.bfloat16)).reshape(
        seg_count, SEG, local_heads, HD
    )
    value_segs = value_n.reshape(seg_count, SEG, local_heads, HD)
    a_mats = jnp.einsum("cthi,cthj->chij", keys_live, keys_live, preferred_element_type=jnp.float32)
    b_mats = jnp.einsum(
        "cthi,cthj->chij", keys_live, value_segs, preferred_element_type=jnp.float32
    )
    my_rates = lax.dynamic_slice_in_dim(memory_rates, group_index * local_heads, local_heads, 2)
    decay_factor = my_rates[0][:, :, None, None]
    eta = my_rates[1][:, :, None, None]
    theta = my_rates[2][:, :, None, None]
    keep = (1 - seg_start).astype(jnp.float32)[:, None, None, None]
    identity = jnp.eye(HD, dtype=jnp.float32)
    upper = jnp.concatenate([(1.0 - decay_factor) * identity - theta * a_mats, eta * identity], -1)
    lower = jnp.concatenate([-theta * a_mats, eta * identity], -1)
    seg_maps = jnp.concatenate([upper, lower], -2) * keep
    seg_shifts = jnp.concatenate([theta * b_mats, theta * b_mats], -2)
    reach = min(PROMPT_SPAN, lax.axis_size("seq"))
    memory_in = memory_entering(seg_maps[0], seg_shifts[0], "seq", reach) * keep[0]
    query_seg = query_n.astype(jnp.float32)
    retr_parts = jnp.einsum("thi,hij->thj", query_seg, memory_in, precision=lax.Precision.HIGHEST)
    mem = retr_parts * lax.rsqrt(jnp.mean(retr_parts * retr_parts, -1, keepdims=True) + epsilon)
    block_rows = SEG
    attn_parts = []
    seg_index = 0
    first = seg_index * SEG
    keys_all = jnp.concatenate([pkeys, key_n], 0)
    values_all = jnp.concatenate([pvalues, value_n], 0)
    cols_k = jnp.arange(persist_rows + SEG, dtype=jnp.int32)[None, :] - persist_rows
    for block_start in range(0, SEG, block_rows):
        query_blk = query_n[first + block_start : first + block_start + block_rows]
        scores = score_scale * jnp.einsum(
            "qhd,khd->hqk", query_blk, keys_all, preferred_element_type=jnp.float32
        )
        rows_q = block_start + jnp.arange(block_rows, dtype=jnp.int32)[:, None]
        allow = (cols_k < 0) | (cols_k <= rows_q) & (cols_k < seg_len[seg_index])
        weights = jnp.where(allow[None], jnp.exp(scores), 0.0)
        probs = (weights / jnp.sum(weights, -1, keepdims=True)).astype(jnp.bfloat16)
        attn_parts.append(
            jnp.einsum("hqk,khd->qhd", probs, values_all, preferred_element_type=jnp.float32)
        )
    attn = jnp.concatenate(attn_parts, 0)
    heads_out = (attn + mem).astype(jnp.bfloat16).reshape(token_rows, head_width)
    chunk = token_rows // FINISH_CHUNKS
    outs = []
    for first_row in range(0, token_rows, chunk):
        rows = slice(first_row, first_row + chunk)
        share = direct_sum(heads_out[rows], w_out, ("tr", "tc"))
        resid = (activations[rows].astype(jnp.float32) + share).astype(jnp.bfloat16)
        (gate, up_proj), squares2 = direct_products(resid, (w_gate, w_up), ("tr", "tc"))
        inv_rms2 = lax.rsqrt(squares2 / full_width + epsilon)[:, None]
        hidden = (jax.nn.silu(gate * inv_rms2) * (up_proj * inv_rms2)).astype(jnp.bfloat16)
        ffn_share = direct_sum(hidden, w_down, ("tr", "tc"))
        outs.append((resid.astype(jnp.float32) + ffn_share).astype(jnp.bfloat16))
    return jnp.concatenate(outs, 0)


def solution(mesh):
    return jax.shard_map(
        body,
        mesh=mesh,
        in_specs=(
            P("seq", ("tr", "tc")),
            P("seq"),
            P("seq"),
            P(None, "seq", None),
            P(None, None, ("tr", "tc")),
            P(None, None, ("tr", "tc")),
            P(None, None, ("tr", "tc")),
            P(("tr", "tc"), None),
            P(None, ("tr", "tc")),
            P(None, ("tr", "tc")),
            P(("tr", "tc"), None),
        ),
        out_specs=P("seq", ("tr", "tc")),
        check_vma=False,
    )
```

```python
import jax
import jax.numpy as jnp
from jax import lax
from jax.sharding import PartitionSpec as P

HD = 128
SEG = 1024
CONV = 4
PROMPT_SPAN = 32
FINISH_CHUNKS = 1


epsilon = 1e-06
score_scale = 8.0


def passed_along(block, axis, distance):
    devices = range(lax.axis_size(axis))
    route = [(i - distance, i) for i in devices if i - distance in devices]
    return lax.ppermute(block, axis, route)


def exact_pair(block):
    high = block.astype(jnp.bfloat16)
    low = (block - high.astype(jnp.float32)).astype(jnp.bfloat16)
    return jnp.concatenate([high, low], -1)


def from_pair(pair):
    half = pair.shape[-1] // 2
    return pair[..., :half].astype(jnp.float32) + pair[..., half:].astype(jnp.float32)


def routed(block, axis, pairs):
    return lax.ppermute(block, axis, [(i, j) for i, j in pairs if 0 <= i])


def memory_entering(seg_map, seg_shift, axis, reach):
    count = lax.axis_size(axis)
    odd = lax.axis_index(axis) % 2 == 1
    width = seg_map.shape[-1]
    rows = seg_shift.shape[-1]
    payload = jnp.concatenate([seg_map, seg_shift], -1).astype(jnp.bfloat16)
    sibling = routed(payload, axis, [(i - 1, i) for i in range(1, count, 2)]).astype(jnp.float32)
    moved = exact_product(seg_map, sibling)
    pair_map = jnp.where(odd, moved[..., :width], seg_map)
    pair_shift = jnp.where(odd, moved[..., width:] + seg_shift, seg_shift)
    chips = 1
    while 4 * chips < reach:
        payload = jnp.concatenate([pair_map, pair_shift], -1).astype(jnp.bfloat16)
        arrived = routed(payload, axis, [(i - 2 * chips, i) for i in range(1, count, 2)])
        moved = exact_product(pair_map, arrived.astype(jnp.float32))
        pair_shift = moved[..., width:] + pair_shift
        pair_map = moved[..., :width]
        chips *= 2
    span = 2 * chips
    far = routed(pair_shift.astype(jnp.bfloat16), axis, [(i - span, i) for i in range(1, count, 2)])
    window = exact_product(pair_map, far.astype(jnp.float32)) + pair_shift
    to_even = from_pair(
        routed(exact_pair(window[:, :rows]), axis, [(i - 1, i) for i in range(2, count, 2)])
    )
    to_odd = from_pair(routed(exact_pair(window), axis, [(i - 2, i) for i in range(3, count, 2)]))
    sibling_map = sibling[..., :width][:, :rows]
    sibling_shift = sibling[..., width:][:, :rows]
    odd_state = exact_product(sibling_map, to_odd) + sibling_shift
    return jnp.where(odd, odd_state, to_even)


def ring_place(index):
    return (index % 2) * 2 + index // 2


def ring_route(axis, step):
    count = lax.axis_size(axis)
    return [(i, ring_place((ring_place(i) + step) % count)) for i in range(count)]


def gathered_products(local, weights, axis):
    count, index = (lax.axis_size(axis), lax.axis_index(axis))
    width = local.shape[1]
    place = ring_place(index)
    half = local.shape[0] // 2
    from_left = lax.ppermute(local, axis, ring_route(axis, 1))
    from_right = lax.ppermute(local, axis, ring_route(axis, -1))
    far_top = lax.ppermute(from_left[:half], axis, ring_route(axis, 1))
    far_bottom = lax.ppermute(from_right[half:], axis, ring_route(axis, -1))
    far = jnp.concatenate([far_top, far_bottom], 0)
    pieces = [
        (local, index),
        (from_left, ring_place((place - 1) % count)),
        (from_right, ring_place((place + 1) % count)),
        (far, ring_place((place + 2) % count)),
    ]
    totals = [None] * len(weights)
    squares = None
    for piece, source in pieces:
        piece_f = piece.astype(jnp.float32)
        part_sq = jnp.sum(piece_f * piece_f, -1)
        squares = part_sq if squares is None else squares + part_sq
        for k, weight in enumerate(weights):
            rows = lax.dynamic_slice_in_dim(weight, source * width, width, 0)
            term = jnp.dot(piece, rows, preferred_element_type=jnp.float32)
            totals[k] = term if totals[k] is None else totals[k] + term
    return totals, squares


def direct_products(local, weights, axis):
    count, index = (lax.axis_size(axis), lax.axis_index(axis))
    width = local.shape[1]
    pieces = [(local, index)]
    for distance in range(1, count):
        route = [(i, (i + distance) % count) for i in range(count)]
        pieces.append((lax.ppermute(local, axis, route), (index - distance) % count))
    totals = [None] * len(weights)
    squares = None
    for piece, source in pieces:
        piece_f = piece.astype(jnp.float32)
        part_sq = jnp.sum(piece_f * piece_f, -1)
        squares = part_sq if squares is None else squares + part_sq
        for k, weight in enumerate(weights):
            rows = lax.dynamic_slice_in_dim(weight, source * width, width, 0)
            term = jnp.dot(piece, rows, preferred_element_type=jnp.float32)
            totals[k] = term if totals[k] is None else totals[k] + term
    return totals, squares


def direct_sum(left, weight, axis):
    count, index = (lax.axis_size(axis), lax.axis_index(axis))
    width = weight.shape[1] // count

    def block(owner):
        cols = lax.dynamic_slice_in_dim(weight, owner * width, width, 1)
        return jnp.dot(left, cols, preferred_element_type=jnp.float32).astype(jnp.bfloat16)

    total = block(index).astype(jnp.float32)
    for distance in range(1, count):
        route = [(i, (i + distance) % count) for i in range(count)]
        arrived = lax.ppermute(block((index + distance) % count), axis, route)
        total = total + arrived.astype(jnp.float32)
    return total


def scattered_sum(left, weight, axis):
    count, index = (lax.axis_size(axis), lax.axis_index(axis))
    width = weight.shape[1] // count
    place = ring_place(index)
    half = left.shape[0] // 2

    def block(owner_place, rows=slice(None)):
        owner = ring_place(owner_place % count)
        cols = lax.dynamic_slice_in_dim(weight, owner * width, width, 1)
        return jnp.dot(left[rows], cols, preferred_element_type=jnp.float32)

    relay_top = lax.ppermute(
        block(place + 2, slice(0, half)).astype(jnp.bfloat16), axis, ring_route(axis, 1)
    )
    relay_bottom = lax.ppermute(
        block(place + 2, slice(half, None)).astype(jnp.bfloat16), axis, ring_route(axis, -1)
    )
    right_block = block(place + 1).astype(jnp.bfloat16).astype(jnp.float32)
    right_block = jnp.concatenate(
        [right_block[:half] + relay_top.astype(jnp.float32), right_block[half:]], 0
    )
    left_block = block(place - 1).astype(jnp.bfloat16).astype(jnp.float32)
    left_block = jnp.concatenate(
        [left_block[:half], left_block[half:] + relay_bottom.astype(jnp.float32)], 0
    )
    from_left = lax.ppermute(right_block.astype(jnp.bfloat16), axis, ring_route(axis, 1))
    from_right = lax.ppermute(left_block.astype(jnp.bfloat16), axis, ring_route(axis, -1))
    own = block(place).astype(jnp.bfloat16).astype(jnp.float32)
    return own + from_left.astype(jnp.float32) + from_right.astype(jnp.float32)


def unit_rows(values_in):
    return values_in * lax.rsqrt(jnp.sum(values_in * values_in, -1, keepdims=True) + epsilon)


def exact_product(left, right):
    return jnp.matmul(left, right, precision=lax.Precision.HIGHEST)


def body(
    activations,
    seg_len,
    seg_start,
    memory_rates,
    w_qkv,
    conv_w,
    persistent,
    w_out,
    w_gate,
    w_up,
    w_down,
):
    token_rows, local_feat = activations.shape
    seg_count = seg_len.shape[0]
    full_width = w_qkv.shape[0]
    head_width = w_qkv.shape[2]
    local_heads = head_width // HD
    group_index = lax.axis_index(("tr", "tc"))
    wide = w_qkv.reshape(full_width, 3 * head_width)
    row_ids = jnp.arange(token_rows, dtype=jnp.int32)
    position = row_ids % SEG
    segment_of = row_ids // SEG
    continuing = seg_start[segment_of] == 0
    (projected,), squares = direct_products(activations, (wide,), ("tr", "tc"))
    qkv = (projected * lax.rsqrt(squares / full_width + epsilon)[:, None]).astype(jnp.bfloat16)
    edge_rows = passed_along(qkv[token_rows - (CONV - 1) :], "seq", 1)
    extended = jnp.concatenate([edge_rows, qkv], 0)
    taps = conv_w.reshape(CONV, 3 * head_width)
    convolved = jnp.zeros((token_rows, 3 * head_width), jnp.float32)
    for offset in range(CONV):
        shifted = extended[CONV - 1 - offset : CONV - 1 - offset + token_rows].astype(jnp.float32)
        valid = (position >= offset) | continuing
        convolved = convolved + jnp.where(valid[:, None], taps[offset] * shifted, 0.0)
    parts = convolved.reshape(token_rows, 3, local_heads, HD)
    query_n = unit_rows(parts[:, 0]).astype(jnp.bfloat16)
    key_n = unit_rows(parts[:, 1]).astype(jnp.bfloat16)
    value_n = parts[:, 2].astype(jnp.bfloat16)
    pkeys = unit_rows(persistent[0].astype(jnp.float32).reshape(-1, local_heads, HD)).astype(
        jnp.bfloat16
    )
    pvalues = persistent[1].reshape(-1, local_heads, HD)
    persist_rows = pkeys.shape[0]
    live = position < seg_len[segment_of]
    keys_live = jnp.where(live[:, None, None], key_n, jnp.zeros((), jnp.bfloat16)).reshape(
        seg_count, SEG, local_heads, HD
    )
    value_segs = value_n.reshape(seg_count, SEG, local_heads, HD)
    a_mats = jnp.einsum("cthi,cthj->chij", keys_live, keys_live, preferred_element_type=jnp.float32)
    b_mats = jnp.einsum(
        "cthi,cthj->chij", keys_live, value_segs, preferred_element_type=jnp.float32
    )
    my_rates = lax.dynamic_slice_in_dim(memory_rates, group_index * local_heads, local_heads, 2)
    decay_factor = my_rates[0][:, :, None, None]
    eta = my_rates[1][:, :, None, None]
    theta = my_rates[2][:, :, None, None]
    keep = (1 - seg_start).astype(jnp.float32)[:, None, None, None]
    identity = jnp.eye(HD, dtype=jnp.float32)
    upper = jnp.concatenate([(1.0 - decay_factor) * identity - theta * a_mats, eta * identity], -1)
    lower = jnp.concatenate([-theta * a_mats, eta * identity], -1)
    seg_maps = jnp.concatenate([upper, lower], -2) * keep
    seg_shifts = jnp.concatenate([theta * b_mats, theta * b_mats], -2)
    reach = min(PROMPT_SPAN, lax.axis_size("seq"))
    memory_in = memory_entering(seg_maps[0], seg_shifts[0], "seq", reach) * keep[0]
    query_seg = query_n.astype(jnp.float32)
    retr_parts = jnp.einsum("thi,hij->thj", query_seg, memory_in, precision=lax.Precision.HIGHEST)
    mem = retr_parts * lax.rsqrt(jnp.mean(retr_parts * retr_parts, -1, keepdims=True) + epsilon)
    block_rows = SEG
    attn_parts = []
    seg_index = 0
    first = seg_index * SEG
    keys_all = jnp.concatenate([pkeys, key_n], 0)
    values_all = jnp.concatenate([pvalues, value_n], 0)
    cols_k = jnp.arange(persist_rows + SEG, dtype=jnp.int32)[None, :] - persist_rows
    for block_start in range(0, SEG, block_rows):
        query_blk = query_n[first + block_start : first + block_start + block_rows]
        scores = score_scale * jnp.einsum(
            "qhd,khd->hqk", query_blk, keys_all, preferred_element_type=jnp.float32
        )
        rows_q = block_start + jnp.arange(block_rows, dtype=jnp.int32)[:, None]
        allow = (cols_k < 0) | (cols_k <= rows_q) & (cols_k < seg_len[seg_index])
        weights = jnp.where(allow[None], jnp.exp(scores), 0.0)
        probs = (weights / jnp.sum(weights, -1, keepdims=True)).astype(jnp.bfloat16)
        attn_parts.append(
            jnp.einsum("hqk,khd->qhd", probs, values_all, preferred_element_type=jnp.float32)
        )
    attn = jnp.concatenate(attn_parts, 0)
    heads_out = (attn + mem).astype(jnp.bfloat16).reshape(token_rows, head_width)
    chunk = token_rows // FINISH_CHUNKS
    outs = []
    for first_row in range(0, token_rows, chunk):
        rows = slice(first_row, first_row + chunk)
        share = direct_sum(heads_out[rows], w_out, ("tr", "tc"))
        resid = (activations[rows].astype(jnp.float32) + share).astype(jnp.bfloat16)
        (gate, up_proj), squares2 = direct_products(resid, (w_gate, w_up), ("tr", "tc"))
        inv_rms2 = lax.rsqrt(squares2 / full_width + epsilon)[:, None]
        hidden = (jax.nn.silu(gate * inv_rms2) * (up_proj * inv_rms2)).astype(jnp.bfloat16)
        ffn_share = direct_sum(hidden, w_down, ("tr", "tc"))
        outs.append((resid.astype(jnp.float32) + ffn_share).astype(jnp.bfloat16))
    return jnp.concatenate(outs, 0)


def solution(mesh):
    return jax.shard_map(
        body,
        mesh=mesh,
        in_specs=(
            P("seq", ("tr", "tc")),
            P("seq"),
            P("seq"),
            P(None, "seq", None),
            P(None, None, ("tr", "tc")),
            P(None, None, ("tr", "tc")),
            P(None, None, ("tr", "tc")),
            P(("tr", "tc"), None),
            P(None, ("tr", "tc")),
            P(None, ("tr", "tc")),
            P(("tr", "tc"), None),
        ),
        out_specs=P("seq", ("tr", "tc")),
        check_vma=False,
    )
```
